256 devices in a mesh: seq: 32 (over z, y), head: 8 (over x, core).
Axes of the slice: x: 4, y: 4, z: 8, core: 2. Of those that a mesh axis runs over, the one named last changes fastest.
Arguments:
- query_proj: bfloat16 [8192, 2048], P('seq', 'head'), may hold values from -40 to 40
- key_proj: bfloat16 [8192, 2048], P('seq', 'head'), may hold values from -40 to 40
- value_proj: bfloat16 [8192, 4096], P('seq', 'head'), may hold values from -40 to 40
- gate_proj: bfloat16 [8192, 4096], P('seq', 'head'), may hold values from -6 to 6
- strength: float32 [32, 8192], P('head', 'seq'), may hold values from 0 to 2, as said below
- log_decay: float32 [32, 8192], P('head', 'seq'), may hold values from -1 to 0, as said below
- conv_query: bfloat16 [4, 2048], P(None, 'head'), may hold values from -3 to 3
- conv_key: bfloat16 [4, 2048], P(None, 'head'), may hold values from -3 to 3
- conv_value: bfloat16 [4, 4096], P(None, 'head'), may hold values from -3 to 3
- norm_gain: bfloat16 [128], replicated, may hold values from 0.099609375 to 1.8984375
- out_weight: bfloat16 [4096, 2048], P('head'), may hold values from -0.09375 to 0.09375
Outputs:
- layer_out: bfloat16 [8192, 2048], P(('seq', 'head'))
The draws below stay inside these ranges and needn't reach their ends.
Inputs may be any that keep to these rules, and one draw needn't show every extreme that they name: `strength`: strictly inside the range. `log_decay`: strictly below the upper end.
All inputs are finite; a program needn't handle non-finite values.
Results may differ from the reference program's by a relative error of at most 0.014.
Values may be sent and summed in bfloat16 or wider, within the bound.
No kernel may reach another device: no remote copies, remote signals or barrier semaphores. Data moves between devices by JAX's collectives and lax.ppermute only.
A program may use at most 64 MiB of HBM per device.

```python
import math
import jax
import jax.numpy as jnp
from jax import lax

D = 2048
HK = 16
HV = 32
DK = 128
DV = 128
KCONV = 4
SPAN = 128
TOK_DEV = 256
SEQUENCE_TOKENS = 8192
N_HEAD = 8


def slow_heads(key):
    head_kinds = jax.random.randint(jax.random.fold_in(key, 101), (HV,), 0, 8)
    fast_cut = 4
    return head_kinds >= fast_cut


def rough_field(key, row_count, col_count, col_spread, early_gain):
    key_base = jax.random.fold_in(key, 1)
    key_rows = jax.random.fold_in(key, 2)
    key_cols = jax.random.fold_in(key, 3)
    base_values = jax.random.truncated_normal(key_base, -4.0, 4.0, (row_count, col_count), jnp.float32)
    row_scale = jnp.exp(jax.random.uniform(key_rows, (row_count, 1), jnp.float32, -1.1, 1.1))
    col_scale = jnp.exp(jax.random.uniform(key_cols, (1, col_count), jnp.float32, -col_spread, col_spread))
    row_index = jnp.arange(row_count)
    early_rows = jnp.where(row_index < row_count // 8, early_gain, 1.0)[:, None]
    return jnp.clip(base_values * row_scale * col_scale * early_rows, -40.0, 40.0)


def draw_query_proj(key, part):
    return rough_field(jax.random.fold_in(key, 21), SEQUENCE_TOKENS, HK * DK, 1.1, 1.0).astype(jnp.bfloat16)


def draw_key_proj(key, part):
    return rough_field(jax.random.fold_in(key, 22), SEQUENCE_TOKENS, HK * DK, 1.4, 1.0).astype(jnp.bfloat16)


def draw_value_proj(key, part):
    return rough_field(jax.random.fold_in(key, 23), SEQUENCE_TOKENS, HV * DV, 1.1, 3.0).astype(jnp.bfloat16)


def draw_strength(key, part):
    slow_mask = slow_heads(key)
    key_level = jax.random.fold_in(key, 31)
    key_jitter = jax.random.fold_in(key, 32)
    key_fast = jax.random.fold_in(key, 33)
    level_low, level_high, fast_low, fast_high = (1.5, 6.0, 0.2, 1.8)
    head_level = jnp.exp(jax.random.uniform(key_level, (HV, 1), jnp.float32, math.log(level_low), math.log(level_high))) * (DK / SEQUENCE_TOKENS)
    jitter = jax.random.uniform(key_jitter, (HV, SEQUENCE_TOKENS), jnp.float32, 0.5, 1.5)
    fast_values = jax.random.uniform(key_fast, (HV, SEQUENCE_TOKENS), jnp.float32, fast_low, fast_high)
    return jnp.where(slow_mask[:, None], jnp.minimum(head_level * jitter, 1.9), fast_values)


def draw_log_decay(key, part):
    slow_mask = slow_heads(key)
    key_fast = jax.random.fold_in(key, 41)
    key_slow = jax.random.fold_in(key, 42)
    key_block = jax.random.fold_in(key, 43)
    key_jitter = jax.random.fold_in(key, 44)
    key_locations = jax.random.fold_in(key, 45)
    key_depth = jax.random.fold_in(key, 46)
    fast_rate = jnp.exp(jax.random.uniform(key_fast, (HV, 1), jnp.float32, math.log(1.0 / 50.0), math.log(1.0 / 30.0)))
    slow_rate = jnp.exp(jax.random.uniform(key_slow, (HV, 1), jnp.float32, math.log(0.2), math.log(0.6))) / SEQUENCE_TOKENS
    blocks = SEQUENCE_TOKENS // TOK_DEV
    block_factor = jnp.exp(jax.random.uniform(key_block, (HV, blocks, 1), jnp.float32, math.log(0.5), math.log(2.0)))
    block_factor = jnp.broadcast_to(block_factor, (HV, blocks, TOK_DEV)).reshape(HV, SEQUENCE_TOKENS)
    jitter = jax.random.uniform(key_jitter, (HV, SEQUENCE_TOKENS), jnp.float32, 0.5, 1.5)
    decay_speed = jnp.where(slow_mask[:, None], slow_rate, fast_rate) * block_factor * jitter
    spike_locations = jax.random.randint(key_locations, (2,), 0, SEQUENCE_TOKENS)
    layer_depths = jax.random.uniform(key_depth, (HV, 2), jnp.float32, math.log(0.5), math.log(0.8))
    column_index = jnp.arange(SEQUENCE_TOKENS)
    spike_events = jnp.where(column_index[None, :] == spike_locations[0], layer_depths[:, 0:1], 0.0)
    spike_events = spike_events + jnp.where(column_index[None, :] == spike_locations[1], layer_depths[:, 1:2], 0.0)
    return spike_events - decay_speed


def level_of(key, extent, pieces, smallest, largest):
    def one(dim, shards_of):
        draws = jax.random.uniform(jax.random.fold_in(jax.random.fold_in(key, 6), dim), (shards_of,), jnp.float32, smallest / len(pieces), largest / len(pieces))
        return jnp.repeat(jnp.exp(draws), extent[dim] // shards_of).reshape((-1,) + (1,) * (len(extent) - dim - 1))

    loudness = one(*pieces[0])
    for cut in pieces[1:]:
        loudness = loudness * one(*cut)
    return loudness


def normal_values(rng, extent, scale, most, shards=(), held_as=jnp.bfloat16):
    entries = scale * jax.random.normal(rng, extent, jnp.float32)
    if shards:
        entries = entries * level_of(rng, extent, shards, -0.22, 0.18)
    return jnp.clip(entries, -most, most).astype(held_as)


def setup_inputs(seed: int = 0) -> dict:
    key_list = jax.random.split(jax.random.key(seed), 12)
    query_proj = draw_query_proj(jax.random.fold_in(key_list[11], 71), 0)
    key_proj = draw_key_proj(jax.random.fold_in(key_list[11], 71), 0)
    value_proj = draw_value_proj(jax.random.fold_in(key_list[11], 71), 0)
    gate_proj = normal_values(key_list[3], (SEQUENCE_TOKENS, HV * DV), 1.0, 6.0, ((0, 32), (1, 8)))
    strength = draw_strength(jax.random.fold_in(key_list[11], 71), 0)
    log_decay = draw_log_decay(jax.random.fold_in(key_list[11], 71), 0)
    conv_query = normal_values(key_list[6], (KCONV, HK * DK), KCONV ** -0.5, 3.0, ((1, 8),))
    conv_key = normal_values(key_list[7], (KCONV, HK * DK), KCONV ** -0.5, 3.0, ((1, 8),))
    conv_value = normal_values(key_list[8], (KCONV, HV * DV), KCONV ** -0.5, 3.0, ((1, 8),))
    norm_gain = jnp.clip(1.0 + 0.18 * jax.random.normal(key_list[9], (DV,), jnp.float32), 0.099609375, 1.8984375).astype(jnp.bfloat16)
    out_weight = normal_values(key_list[10], (HV * DV, D), (HV * DV) ** -0.5, 0.09375, ((0, 8),))
    return dict(query_proj=query_proj, key_proj=key_proj, value_proj=value_proj, gate_proj=gate_proj, strength=strength, log_decay=log_decay, conv_query=conv_query, conv_key=conv_key, conv_value=conv_value, norm_gain=norm_gain, out_weight=out_weight)


epsilon = 1e-06
highest = lax.Precision.HIGHEST

def conv_silu(signal, weights):
    length = signal.shape[0]
    padded = jnp.concatenate([jnp.zeros((KCONV - 1, signal.shape[1]), jnp.float32), signal.astype(jnp.float32)], axis=0)
    conv_taps = weights.astype(jnp.float32)
    summed = jnp.zeros((length, signal.shape[1]), jnp.float32)
    for offset in range(KCONV):
        summed = summed + conv_taps[offset] * padded[offset:offset + length]
    return jax.nn.silu(summed)

def advance(state_now, span_in):
    query_span, key_span, value_span, strength_span, decay_span = span_in
    cumulative = jnp.cumsum(decay_span, axis=-1)
    positions = jnp.arange(SPAN)
    inclusive = positions[:, None] >= positions[None, :]
    strictly = positions[:, None] > positions[None, :]
    log_gaps = cumulative[:, :, None] - cumulative[:, None, :]
    decays = jnp.where(inclusive, jnp.exp(jnp.where(inclusive, log_gaps, 0.0)), 0.0)
    key_key = jnp.dot(key_span, key_span.T, precision=highest)
    query_key = jnp.dot(query_span, key_span.T, precision=highest)
    lower_part = jnp.where(strictly, strength_span[:, :, None] * decays * key_key[None], 0.0)
    system = lower_part + jnp.eye(SPAN, dtype=jnp.float32)
    right_side = jnp.concatenate([strength_span[:, :, None] * value_span, (strength_span * jnp.exp(cumulative))[:, :, None] * key_span[None]], axis=-1)
    solved = lax.linalg.triangular_solve(system, right_side, left_side=True, lower=True, unit_diagonal=True)
    written = solved[..., :DV] - jnp.einsum('rck,rkv->rcv', solved[..., DV:], state_now, precision=highest)
    attention = decays * query_key[None]
    outputs = jnp.einsum('rck,rkv->rcv', jnp.exp(cumulative)[:, :, None] * query_span[None], state_now, precision=highest)
    outputs = outputs + jnp.einsum('rce,rev->rcv', attention, written, precision=highest)
    span_end = cumulative[:, -1:]
    scaled_keys = jnp.exp(span_end - cumulative)[:, :, None] * key_span[None]
    state_next = jnp.exp(span_end)[:, :, None] * state_now + jnp.einsum('rck,rcv->rkv', scaled_keys, written, precision=highest)
    return (state_next, outputs)

def reference(query_proj, key_proj, value_proj, gate_proj, strength, log_decay, conv_query, conv_key, conv_value, norm_gain, out_weight):
    ratio_heads = HV // HK
    group_width = ratio_heads * DV
    spans = SEQUENCE_TOKENS // SPAN
    gain_values = norm_gain.astype(jnp.float32)

    def head_core(packed):
        query_raw, key_raw, value_raw, gate_raw, strength_head, decay_head, query_taps, key_taps, value_taps = packed
        queries = conv_silu(query_raw, query_taps)
        key_rows = conv_silu(key_raw, key_taps)
        key_rows = key_rows / jnp.sqrt(lax.optimization_barrier(jnp.sum(key_rows * key_rows, axis=-1, keepdims=True)) + epsilon)
        values = conv_silu(value_raw, value_taps)
        query_blocks = queries.reshape(spans, SPAN, DK)
        key_blocks = key_rows.reshape(spans, SPAN, DK)
        value_blocks = values.reshape(spans, SPAN, ratio_heads, DV).transpose(0, 2, 1, 3)
        strength_blocks = strength_head.reshape(ratio_heads, spans, SPAN).transpose(1, 0, 2)
        decay_blocks = decay_head.reshape(ratio_heads, spans, SPAN).transpose(1, 0, 2)
        zero_state = jnp.zeros((ratio_heads, DK, DV), jnp.float32)
        ignored, outputs = lax.scan(advance, zero_state, (query_blocks, key_blocks, value_blocks, strength_blocks, decay_blocks))
        core_out = outputs.transpose(0, 2, 1, 3).reshape(SEQUENCE_TOKENS, ratio_heads, DV)
        gate_values = gate_raw.astype(jnp.float32).reshape(SEQUENCE_TOKENS, ratio_heads, DV)
        scale_rows = lax.rsqrt(lax.optimization_barrier(jnp.mean(core_out * core_out, axis=-1, keepdims=True)) + epsilon)
        normed = core_out * scale_rows * gain_values * jax.nn.silu(gate_values)
        return normed.reshape(SEQUENCE_TOKENS, group_width).astype(jnp.bfloat16)
    query_stack = query_proj.reshape(SEQUENCE_TOKENS, HK, DK).transpose(1, 0, 2)
    key_stack = key_proj.reshape(SEQUENCE_TOKENS, HK, DK).transpose(1, 0, 2)
    value_stack = value_proj.reshape(SEQUENCE_TOKENS, HK, group_width).transpose(1, 0, 2)
    gate_stack = gate_proj.reshape(SEQUENCE_TOKENS, HK, group_width).transpose(1, 0, 2)
    strength_stack = strength.reshape(HK, ratio_heads, SEQUENCE_TOKENS)
    decay_stack = log_decay.reshape(HK, ratio_heads, SEQUENCE_TOKENS)
    query_taps = conv_query.reshape(KCONV, HK, DK).transpose(1, 0, 2)
    key_taps = conv_key.reshape(KCONV, HK, DK).transpose(1, 0, 2)
    value_taps = conv_value.reshape(KCONV, HK, group_width).transpose(1, 0, 2)
    hidden = lax.map(head_core, (query_stack, key_stack, value_stack, gate_stack, strength_stack, decay_stack, query_taps, key_taps, value_taps))
    hidden = hidden.transpose(1, 0, 2).reshape(SEQUENCE_TOKENS, HV * DV)
    group_cols = HV * DV // N_HEAD
    summed = jnp.zeros((SEQUENCE_TOKENS, D), jnp.float32)
    for group in range(N_HEAD):
        lower_col = group * group_cols
        partial_sum = jnp.dot(hidden[:, lower_col:lower_col + group_cols].astype(jnp.float32), out_weight[lower_col:lower_col + group_cols].astype(jnp.float32), preferred_element_type=jnp.float32).astype(jnp.bfloat16)
        summed = summed + lax.optimization_barrier(partial_sum).astype(jnp.float32)
    return summed.astype(jnp.bfloat16)
```

```python
import jax
import jax.numpy as jnp
from jax import lax
from jax.sharding import PartitionSpec as P

DK = 128
DV = 128
SPAN = 128


epsilon = 1e-06
highest = lax.Precision.HIGHEST


def shifted(array, axis, by):
    length = lax.axis_size(axis)
    pairs = [(i, i + by) for i in range(length) if 0 <= i + by < length]
    return lax.ppermute(array, axis, pairs)


def conv_silu(signal, before, weights):
    length = signal.shape[0]
    padded = jnp.concatenate([before, signal], axis=0).astype(jnp.float32)
    conv_taps = weights.astype(jnp.float32)
    summed = jnp.zeros(signal.shape, jnp.float32)
    for offset in range(conv_taps.shape[0]):
        summed = summed + conv_taps[offset] * padded[offset : offset + length]
    return jax.nn.silu(summed)


def apply_map(matrix, state_now):
    return jnp.einsum("hrke,hrev->hrkv", matrix, state_now, precision=highest)


def shards(
    query_proj,
    key_proj,
    value_proj,
    gate_proj,
    strength,
    log_decay,
    conv_query,
    conv_key,
    conv_value,
    norm_gain,
    out_weight,
):
    local_rows = query_proj.shape[0]
    rim_width = conv_query.shape[0] - 1
    before_query, before_key, before_value = shifted(
        (
            query_proj[local_rows - rim_width :],
            key_proj[local_rows - rim_width :],
            value_proj[local_rows - rim_width :],
        ),
        "seq",
        1,
    )
    key_heads = key_proj.shape[1] // DK
    value_heads = value_proj.shape[1] // DV
    ratio_heads = value_heads // key_heads
    spans = local_rows // SPAN
    queries = conv_silu(query_proj, before_query, conv_query)
    key_rows = conv_silu(key_proj, before_key, conv_key).reshape(local_rows, key_heads, DK)
    key_rows = key_rows / jnp.sqrt(jnp.sum(key_rows * key_rows, axis=-1, keepdims=True) + epsilon)
    values = conv_silu(value_proj, before_value, conv_value)
    query_blocks = queries.reshape(spans, SPAN, key_heads, DK).transpose(2, 0, 1, 3)[:, None]
    key_blocks = key_rows.reshape(spans, SPAN, key_heads, DK).transpose(2, 0, 1, 3)[:, None]
    value_blocks = values.reshape(spans, SPAN, key_heads, ratio_heads, DV).transpose(2, 3, 0, 1, 4)
    strength_blocks = strength.reshape(key_heads, ratio_heads, spans, SPAN)
    decay_blocks = log_decay.reshape(key_heads, ratio_heads, spans, SPAN)
    cumulative = jnp.cumsum(decay_blocks, axis=-1)
    positions = jnp.arange(SPAN)
    inclusive = positions[:, None] >= positions[None, :]
    strictly = positions[:, None] > positions[None, :]
    log_gaps = cumulative[..., :, None] - cumulative[..., None, :]
    decays = jnp.where(inclusive, jnp.exp(jnp.where(inclusive, log_gaps, 0.0)), 0.0)
    key_key = jnp.einsum("hxnck,hxnek->hxnce", key_blocks, key_blocks, precision=highest)
    query_key = jnp.einsum("hxnck,hxnek->hxnce", query_blocks, key_blocks, precision=highest)
    lower_part = jnp.where(strictly, strength_blocks[..., None] * decays * key_key, 0.0)
    system = lower_part + jnp.eye(SPAN, dtype=jnp.float32)
    right_side = jnp.concatenate(
        [
            strength_blocks[..., None] * value_blocks,
            (strength_blocks * jnp.exp(cumulative))[..., None] * key_blocks,
        ],
        axis=-1,
    )
    solved = lax.linalg.triangular_solve(
        system, right_side, left_side=True, lower=True, unit_diagonal=True
    )
    value_part = solved[..., :DV]
    key_part = solved[..., DV:]
    attention = decays * query_key
    local_out = jnp.einsum("hrnce,hrnev->hrncv", attention, value_part, precision=highest)
    coupling = jnp.exp(cumulative)[..., None] * query_blocks - jnp.einsum(
        "hrnce,hrnek->hrnck", attention, key_part, precision=highest
    )
    span_end = cumulative[..., -1:]
    scaled_keys = jnp.exp(span_end - cumulative)[..., None] * key_blocks
    transit = jnp.exp(span_end)[..., None] * jnp.eye(DK, dtype=jnp.float32) - jnp.einsum(
        "hrnck,hrnce->hrnke", scaled_keys, key_part, precision=highest
    )
    inject = jnp.einsum("hrnck,hrncv->hrnkv", scaled_keys, value_part, precision=highest)
    transit_seq = jnp.moveaxis(transit, 2, 0)
    inject_seq = jnp.moveaxis(inject, 2, 0)
    identity = jnp.broadcast_to(jnp.eye(DK, dtype=jnp.float32), (key_heads, ratio_heads, DK, DK))
    zero_state = jnp.zeros((key_heads, ratio_heads, DK, DV), jnp.float32)

    def sweep_spans(carried, span_in):
        prefix, state_now = carried
        transit_now, inject_now = span_in
        return (
            (apply_map(transit_now, prefix), apply_map(transit_now, state_now) + inject_now),
            None,
        )

    (total_map, local_end), ignored = lax.scan(
        sweep_spans, (identity, zero_state), (transit_seq, inject_seq)
    )

    seq_size = lax.axis_size("seq")
    seq_index = lax.axis_index("seq")
    prefix_map, prefix_end = total_map, local_end
    distance = 1
    while distance < seq_size:
        if 2 * distance < seq_size:
            earlier_map, earlier_end = shifted((prefix_map, prefix_end), "seq", distance)
            prefix_end = apply_map(prefix_map, earlier_end) + prefix_end
            prefix_map = jnp.where(
                seq_index >= distance, apply_map(prefix_map, earlier_map), prefix_map
            )
        else:
            earlier_end = shifted(prefix_end, "seq", distance)
            prefix_end = apply_map(prefix_map, earlier_end) + prefix_end
        distance *= 2
    incoming = shifted(prefix_end, "seq", 1)

    def replay(state_now, span_in):
        transit_now, inject_now, coupling_now, local_now = span_in
        span_out = (
            jnp.einsum("hrck,hrkv->hrcv", coupling_now, state_now, precision=highest) + local_now
        )
        return (apply_map(transit_now, state_now) + inject_now, span_out)

    ignored_state, outputs = lax.scan(
        replay,
        incoming,
        (transit_seq, inject_seq, jnp.moveaxis(coupling, 2, 0), jnp.moveaxis(local_out, 2, 0)),
    )
    core_out = jnp.moveaxis(outputs, 0, 2)
    core_out = core_out.transpose(2, 3, 0, 1, 4).reshape(local_rows, value_heads, DV)
    gate_values = gate_proj.astype(jnp.float32).reshape(local_rows, value_heads, DV)
    scale_rows = lax.rsqrt(jnp.mean(core_out * core_out, axis=-1, keepdims=True) + epsilon)
    normed = core_out * scale_rows * norm_gain.astype(jnp.float32) * jax.nn.silu(gate_values)
    hidden = normed.reshape(local_rows, value_heads * DV).astype(jnp.bfloat16)
    return lax.psum_scatter(
        jnp.dot(hidden, out_weight, preferred_element_type=jnp.float32).astype(jnp.bfloat16),
        "head",
        scatter_dimension=0,
        tiled=True,
    )


def solution(mesh):
    placed = (
        P("seq", "head"),
        P("seq", "head"),
        P("seq", "head"),
        P("seq", "head"),
        P("head", "seq"),
        P("head", "seq"),
        P(None, "head"),
        P(None, "head"),
        P(None, "head"),
        P(),
        P("head", None),
    )
    return jax.shard_map(
        shards, mesh=mesh, in_specs=placed, out_specs=P(("seq", "head"), None), check_vma=False
    )
```

```python
import jax
import jax.numpy as jnp
from jax import lax
from jax.sharding import PartitionSpec as P

DK = 128
DV = 128
SPAN = 128


epsilon = 1e-06
highest = lax.Precision.HIGHEST


def shifted(array, axis, by):
    length = lax.axis_size(axis)
    pairs = [(i, i + by) for i in range(length) if 0 <= i + by < length]
    return lax.ppermute(array, axis, pairs)


def conv_silu(signal, before, weights):
    length = signal.shape[0]
    padded = jnp.concatenate([before, signal], axis=0).astype(jnp.float32)
    conv_taps = weights.astype(jnp.float32)
    summed = jnp.zeros(signal.shape, jnp.float32)
    for offset in range(conv_taps.shape[0]):
        summed = summed + conv_taps[offset] * padded[offset : offset + length]
    return jax.nn.silu(summed)


def unit_lower_inverse(system):
    size = system.shape[-1]
    rows = jnp.arange(size)[:, None]
    cols = jnp.arange(size)[None, :]
    inverse = jnp.broadcast_to(jnp.eye(size, dtype=system.dtype), system.shape)
    width = 1
    while width < size:
        same_block = (rows // (2 * width)) == (cols // (2 * width))
        lower_half = (rows // width) > (cols // width)
        coupling = jnp.where(same_block & lower_half, system, 0.0)
        correction = jnp.einsum(
            "...ij,...jk->...ik",
            jnp.einsum("...ij,...jk->...ik", inverse, coupling, precision=highest),
            inverse,
            precision=highest,
        )
        inverse = jnp.where(same_block & lower_half, -correction, inverse)
        width *= 2
    return inverse


def apply_map(matrix, state_now):
    return jnp.einsum("hrke,hrev->hrkv", matrix, state_now, precision=highest)


def shards(
    query_proj,
    key_proj,
    value_proj,
    gate_proj,
    strength,
    log_decay,
    conv_query,
    conv_key,
    conv_value,
    norm_gain,
    out_weight,
):
    local_rows = query_proj.shape[0]
    rim_width = conv_query.shape[0] - 1
    before_query, before_key, before_value = shifted(
        (
            query_proj[local_rows - rim_width :],
            key_proj[local_rows - rim_width :],
            value_proj[local_rows - rim_width :],
        ),
        "seq",
        1,
    )
    key_heads = key_proj.shape[1] // DK
    value_heads = value_proj.shape[1] // DV
    ratio_heads = value_heads // key_heads
    spans = local_rows // SPAN
    queries = conv_silu(query_proj, before_query, conv_query)
    key_rows = conv_silu(key_proj, before_key, conv_key).reshape(local_rows, key_heads, DK)
    key_rows = key_rows / jnp.sqrt(jnp.sum(key_rows * key_rows, axis=-1, keepdims=True) + epsilon)
    values = conv_silu(value_proj, before_value, conv_value)
    query_blocks = queries.reshape(spans, SPAN, key_heads, DK).transpose(2, 0, 1, 3)[:, None]
    key_blocks = key_rows.reshape(spans, SPAN, key_heads, DK).transpose(2, 0, 1, 3)[:, None]
    value_blocks = values.reshape(spans, SPAN, key_heads, ratio_heads, DV).transpose(2, 3, 0, 1, 4)
    strength_blocks = strength.reshape(key_heads, ratio_heads, spans, SPAN)
    decay_blocks = log_decay.reshape(key_heads, ratio_heads, spans, SPAN)
    cumulative = jnp.cumsum(decay_blocks, axis=-1)
    positions = jnp.arange(SPAN)
    inclusive = positions[:, None] >= positions[None, :]
    strictly = positions[:, None] > positions[None, :]
    log_gaps = cumulative[..., :, None] - cumulative[..., None, :]
    decays = jnp.where(inclusive, jnp.exp(jnp.where(inclusive, log_gaps, 0.0)), 0.0)
    key_key = jnp.einsum("hxnck,hxnek->hxnce", key_blocks, key_blocks, precision=highest)
    query_key = jnp.einsum("hxnck,hxnek->hxnce", query_blocks, key_blocks, precision=highest)
    lower_part = jnp.where(strictly, strength_blocks[..., None] * decays * key_key, 0.0)
    system = lower_part + jnp.eye(SPAN, dtype=jnp.float32)
    right_side = jnp.concatenate(
        [
            strength_blocks[..., None] * value_blocks,
            (strength_blocks * jnp.exp(cumulative))[..., None] * key_blocks,
        ],
        axis=-1,
    )
    solved = jnp.einsum(
        "...ij,...jk->...ik", unit_lower_inverse(system), right_side, precision=highest
    )
    value_part = solved[..., :DV]
    key_part = solved[..., DV:]
    attention = decays * query_key
    local_out = jnp.einsum("hrnce,hrnev->hrncv", attention, value_part, precision=highest)
    coupling = jnp.exp(cumulative)[..., None] * query_blocks - jnp.einsum(
        "hrnce,hrnek->hrnck", attention, key_part, precision=highest
    )
    span_end = cumulative[..., -1:]
    scaled_keys = jnp.exp(span_end - cumulative)[..., None] * key_blocks
    transit = jnp.exp(span_end)[..., None] * jnp.eye(DK, dtype=jnp.float32) - jnp.einsum(
        "hrnck,hrnce->hrnke", scaled_keys, key_part, precision=highest
    )
    inject = jnp.einsum("hrnck,hrncv->hrnkv", scaled_keys, value_part, precision=highest)
    transit_seq = jnp.moveaxis(transit, 2, 0)
    inject_seq = jnp.moveaxis(inject, 2, 0)
    identity = jnp.broadcast_to(jnp.eye(DK, dtype=jnp.float32), (key_heads, ratio_heads, DK, DK))
    zero_state = jnp.zeros((key_heads, ratio_heads, DK, DV), jnp.float32)

    def sweep_spans(carried, span_in):
        prefix, state_now = carried
        transit_now, inject_now = span_in
        return (
            (apply_map(transit_now, prefix), apply_map(transit_now, state_now) + inject_now),
            None,
        )

    (total_map, local_end), ignored = lax.scan(
        sweep_spans, (identity, zero_state), (transit_seq, inject_seq)
    )

    seq_size = lax.axis_size("seq")
    seq_index = lax.axis_index("seq")
    prefix_map, prefix_end = total_map, local_end
    distance = 1
    while distance < seq_size:
        if 2 * distance < seq_size:
            earlier_map, earlier_end = shifted((prefix_map, prefix_end), "seq", distance)
            prefix_end = apply_map(prefix_map, earlier_end) + prefix_end
            prefix_map = jnp.where(
                seq_index >= distance, apply_map(prefix_map, earlier_map), prefix_map
            )
        else:
            earlier_end = shifted(prefix_end, "seq", distance)
            prefix_end = apply_map(prefix_map, earlier_end) + prefix_end
        distance *= 2
    incoming = shifted(prefix_end, "seq", 1)

    def replay(state_now, span_in):
        transit_now, inject_now, coupling_now, local_now = span_in
        span_out = (
            jnp.einsum("hrck,hrkv->hrcv", coupling_now, state_now, precision=highest) + local_now
        )
        return (apply_map(transit_now, state_now) + inject_now, span_out)

    ignored_state, outputs = lax.scan(
        replay,
        incoming,
        (transit_seq, inject_seq, jnp.moveaxis(coupling, 2, 0), jnp.moveaxis(local_out, 2, 0)),
    )
    core_out = jnp.moveaxis(outputs, 0, 2)
    core_out = core_out.transpose(2, 3, 0, 1, 4).reshape(local_rows, value_heads, DV)
    gate_values = gate_proj.astype(jnp.float32).reshape(local_rows, value_heads, DV)
    scale_rows = lax.rsqrt(jnp.mean(core_out * core_out, axis=-1, keepdims=True) + epsilon)
    normed = core_out * scale_rows * norm_gain.astype(jnp.float32) * jax.nn.silu(gate_values)
    hidden = normed.reshape(local_rows, value_heads * DV).astype(jnp.bfloat16)
    return lax.psum_scatter(
        jnp.dot(hidden, out_weight, preferred_element_type=jnp.float32).astype(jnp.bfloat16),
        "head",
        scatter_dimension=0,
        tiled=True,
    )


def solution(mesh):
    placed = (
        P("seq", "head"),
        P("seq", "head"),
        P("seq", "head"),
        P("seq", "head"),
        P("head", "seq"),
        P("head", "seq"),
        P(None, "head"),
        P(None, "head"),
        P(None, "head"),
        P(),
        P("head", None),
    )
    return jax.shard_map(
        shards, mesh=mesh, in_specs=placed, out_specs=P(("seq", "head"), None), check_vma=False
    )
```

```python
import jax
import jax.numpy as jnp
from jax import lax
from jax.sharding import PartitionSpec as P

DK = 128
DV = 128
SPAN = 128


epsilon = 1e-06
highest = lax.Precision.HIGHEST


def shifted(array, axis, by):
    length = lax.axis_size(axis)
    pairs = [(i, i + by) for i in range(length) if 0 <= i + by < length]
    return lax.ppermute(array, axis, pairs)


def conv_silu(signal, before, weights):
    length = signal.shape[0]
    padded = jnp.concatenate([before, signal], axis=0).astype(jnp.float32)
    conv_taps = weights.astype(jnp.float32)
    summed = jnp.zeros(signal.shape, jnp.float32)
    for offset in range(conv_taps.shape[0]):
        summed = summed + conv_taps[offset] * padded[offset : offset + length]
    return jax.nn.silu(summed)


def unit_lower_inverse(system):
    size = system.shape[-1]
    rows = jnp.arange(size)[:, None]
    cols = jnp.arange(size)[None, :]
    inverse = jnp.broadcast_to(jnp.eye(size, dtype=system.dtype), system.shape)
    width = 1
    while width < size:
        same_block = (rows // (2 * width)) == (cols // (2 * width))
        lower_half = (rows // width) > (cols // width)
        coupling = jnp.where(same_block & lower_half, system, 0.0)
        correction = jnp.einsum(
            "...ij,...jk->...ik",
            jnp.einsum("...ij,...jk->...ik", inverse, coupling, precision=highest),
            inverse,
            precision=highest,
        )
        inverse = jnp.where(same_block & lower_half, -correction, inverse)
        width *= 2
    return inverse


def apply_map(matrix, state_now):
    return jnp.einsum("hrke,hrev->hrkv", matrix, state_now, precision=highest)


def shards(
    query_proj,
    key_proj,
    value_proj,
    gate_proj,
    strength,
    log_decay,
    conv_query,
    conv_key,
    conv_value,
    norm_gain,
    out_weight,
):
    local_rows = query_proj.shape[0]
    rim_width = conv_query.shape[0] - 1
    before_query, before_key, before_value = shifted(
        (
            query_proj[local_rows - rim_width :],
            key_proj[local_rows - rim_width :],
            value_proj[local_rows - rim_width :],
        ),
        "seq",
        1,
    )
    key_heads = key_proj.shape[1] // DK
    value_heads = value_proj.shape[1] // DV
    ratio_heads = value_heads // key_heads
    spans = local_rows // SPAN
    queries = conv_silu(query_proj, before_query, conv_query)
    key_rows = conv_silu(key_proj, before_key, conv_key).reshape(local_rows, key_heads, DK)
    key_rows = key_rows / jnp.sqrt(jnp.sum(key_rows * key_rows, axis=-1, keepdims=True) + epsilon)
    values = conv_silu(value_proj, before_value, conv_value)
    query_blocks = queries.reshape(spans, SPAN, key_heads, DK).transpose(2, 0, 1, 3)[:, None]
    key_blocks = key_rows.reshape(spans, SPAN, key_heads, DK).transpose(2, 0, 1, 3)[:, None]
    value_blocks = values.reshape(spans, SPAN, key_heads, ratio_heads, DV).transpose(2, 3, 0, 1, 4)
    strength_blocks = strength.reshape(key_heads, ratio_heads, spans, SPAN)
    decay_blocks = log_decay.reshape(key_heads, ratio_heads, spans, SPAN)
    cumulative = jnp.cumsum(decay_blocks, axis=-1)
    positions = jnp.arange(SPAN)
    inclusive = positions[:, None] >= positions[None, :]
    strictly = positions[:, None] > positions[None, :]
    log_gaps = cumulative[..., :, None] - cumulative[..., None, :]
    decays = jnp.where(inclusive, jnp.exp(jnp.where(inclusive, log_gaps, 0.0)), 0.0)
    key_key = jnp.einsum("hxnck,hxnek->hxnce", key_blocks, key_blocks, precision=highest)
    query_key = jnp.einsum("hxnck,hxnek->hxnce", query_blocks, key_blocks, precision=highest)
    lower_part = jnp.where(strictly, strength_blocks[..., None] * decays * key_key, 0.0)
    system = lower_part + jnp.eye(SPAN, dtype=jnp.float32)
    right_side = jnp.concatenate(
        [
            strength_blocks[..., None] * value_blocks,
            (strength_blocks * jnp.exp(cumulative))[..., None] * key_blocks,
        ],
        axis=-1,
    )
    solved = jnp.einsum(
        "...ij,...jk->...ik", unit_lower_inverse(system), right_side, precision=highest
    )
    value_part = solved[..., :DV]
    key_part = solved[..., DV:]
    attention = decays * query_key
    local_out = jnp.einsum("hrnce,hrnev->hrncv", attention, value_part, precision=highest)
    coupling = jnp.exp(cumulative)[..., None] * query_blocks - jnp.einsum(
        "hrnce,hrnek->hrnck", attention, key_part, precision=highest
    )
    span_end = cumulative[..., -1:]
    scaled_keys = jnp.exp(span_end - cumulative)[..., None] * key_blocks
    transit = jnp.exp(span_end)[..., None] * jnp.eye(DK, dtype=jnp.float32) - jnp.einsum(
        "hrnck,hrnce->hrnke", scaled_keys, key_part, precision=highest
    )
    inject = jnp.einsum("hrnck,hrncv->hrnkv", scaled_keys, value_part, precision=highest)
    transit_seq = jnp.moveaxis(transit, 2, 0)
    inject_seq = jnp.moveaxis(inject, 2, 0)
    identity = jnp.broadcast_to(jnp.eye(DK, dtype=jnp.float32), (key_heads, ratio_heads, DK, DK))
    zero_state = jnp.zeros((key_heads, ratio_heads, DK, DV), jnp.float32)

    def sweep_spans(carried, span_in):
        prefix, state_now = carried
        transit_now, inject_now = span_in
        return (
            (apply_map(transit_now, prefix), apply_map(transit_now, state_now) + inject_now),
            None,
        )

    (total_map, local_end), ignored = lax.scan(
        sweep_spans, (identity, zero_state), (transit_seq, inject_seq)
    )

    seq_size = lax.axis_size("seq")
    seq_index = lax.axis_index("seq")
    prefix_map, prefix_end = total_map, local_end
    distance = 1
    while distance < seq_size:
        if 2 * distance < seq_size:
            earlier_map, earlier_end = shifted(
                jnp.stack([prefix_map, prefix_end]), "seq", distance
            )
            prefix_end = apply_map(prefix_map, earlier_end) + prefix_end
            prefix_map = jnp.where(
                seq_index >= distance, apply_map(prefix_map, earlier_map), prefix_map
            )
        else:
            earlier_end = shifted(prefix_end, "seq", distance)
            prefix_end = apply_map(prefix_map, earlier_end) + prefix_end
        distance *= 2
    incoming = shifted(prefix_end, "seq", 1)

    def replay(state_now, span_in):
        transit_now, inject_now, coupling_now, local_now = span_in
        span_out = (
            jnp.einsum("hrck,hrkv->hrcv", coupling_now, state_now, precision=highest) + local_now
        )
        return (apply_map(transit_now, state_now) + inject_now, span_out)

    ignored_state, outputs = lax.scan(
        replay,
        incoming,
        (transit_seq, inject_seq, jnp.moveaxis(coupling, 2, 0), jnp.moveaxis(local_out, 2, 0)),
    )
    core_out = jnp.moveaxis(outputs, 0, 2)
    core_out = core_out.transpose(2, 3, 0, 1, 4).reshape(local_rows, value_heads, DV)
    gate_values = gate_proj.astype(jnp.float32).reshape(local_rows, value_heads, DV)
    scale_rows = lax.rsqrt(jnp.mean(core_out * core_out, axis=-1, keepdims=True) + epsilon)
    normed = core_out * scale_rows * norm_gain.astype(jnp.float32) * jax.nn.silu(gate_values)
    hidden = normed.reshape(local_rows, value_heads * DV).astype(jnp.bfloat16)
    partial_sum = jnp.dot(hidden, out_weight, preferred_element_type=jnp.float32).astype(
        jnp.bfloat16
    )
    head_size = lax.axis_size("head")
    pieces = lax.all_to_all(
        partial_sum.reshape(head_size, local_rows // head_size, partial_sum.shape[1]),
        "head",
        0,
        0,
    )
    return jnp.sum(pieces.astype(jnp.float32), axis=0).astype(jnp.bfloat16)


def solution(mesh):
    placed = (
        P("seq", "head"),
        P("seq", "head"),
        P("seq", "head"),
        P("seq", "head"),
        P("head", "seq"),
        P("head", "seq"),
        P(None, "head"),
        P(None, "head"),
        P(None, "head"),
        P(),
        P("head", None),
    )
    return jax.shard_map(
        shards, mesh=mesh, in_specs=placed, out_specs=P(("seq", "head"), None), check_vma=False
    )
```

```python
import jax
import jax.numpy as jnp
from jax import lax
from jax.sharding import PartitionSpec as P

DK = 128
DV = 128
SPAN = 128


epsilon = 1e-06
highest = lax.Precision.HIGHEST


def shifted(array, axis, by):
    length = lax.axis_size(axis)
    pairs = [(i, i + by) for i in range(length) if 0 <= i + by < length]
    return lax.ppermute(array, axis, pairs)


def conv_silu(signal, before, weights):
    length = signal.shape[0]
    padded = jnp.concatenate([before, signal], axis=0).astype(jnp.float32)
    conv_taps = weights.astype(jnp.float32)
    summed = jnp.zeros(signal.shape, jnp.float32)
    for offset in range(conv_taps.shape[0]):
        summed = summed + conv_taps[offset] * padded[offset : offset + length]
    return jax.nn.silu(summed)


def unit_lower_inverse(system):
    size = system.shape[-1]
    rows = jnp.arange(size)[:, None]
    cols = jnp.arange(size)[None, :]
    inverse = jnp.broadcast_to(jnp.eye(size, dtype=system.dtype), system.shape)
    width = 1
    while width < size:
        same_block = (rows // (2 * width)) == (cols // (2 * width))
        lower_half = (rows // width) > (cols // width)
        coupling = jnp.where(same_block & lower_half, system, 0.0)
        correction = jnp.einsum(
            "...ij,...jk->...ik",
            jnp.einsum("...ij,...jk->...ik", inverse, coupling, precision=highest),
            inverse,
            precision=highest,
        )
        inverse = jnp.where(same_block & lower_half, -correction, inverse)
        width *= 2
    return inverse


def apply_map(matrix, state_now):
    return jnp.einsum("hrke,hrev->hrkv", matrix, state_now, precision=highest)


def recurrence(query_blocks, key_blocks, value_blocks, strength_blocks, decay_blocks):
    key_heads, ratio_heads = value_blocks.shape[:2]
    cumulative = jnp.cumsum(decay_blocks, axis=-1)
    positions = jnp.arange(SPAN)
    inclusive = positions[:, None] >= positions[None, :]
    strictly = positions[:, None] > positions[None, :]
    log_gaps = cumulative[..., :, None] - cumulative[..., None, :]
    decays = jnp.where(inclusive, jnp.exp(jnp.where(inclusive, log_gaps, 0.0)), 0.0)
    key_key = jnp.einsum("hxnck,hxnek->hxnce", key_blocks, key_blocks, precision=highest)
    query_key = jnp.einsum("hxnck,hxnek->hxnce", query_blocks, key_blocks, precision=highest)
    lower_part = jnp.where(strictly, strength_blocks[..., None] * decays * key_key, 0.0)
    system = lower_part + jnp.eye(SPAN, dtype=jnp.float32)
    right_side = jnp.concatenate(
        [
            strength_blocks[..., None] * value_blocks,
            (strength_blocks * jnp.exp(cumulative))[..., None] * key_blocks,
        ],
        axis=-1,
    )
    solved = jnp.einsum(
        "...ij,...jk->...ik", unit_lower_inverse(system), right_side, precision=highest
    )
    value_part = solved[..., :DV]
    key_part = solved[..., DV:]
    attention = decays * query_key
    local_out = jnp.einsum("hrnce,hrnev->hrncv", attention, value_part, precision=highest)
    coupling = jnp.exp(cumulative)[..., None] * query_blocks - jnp.einsum(
        "hrnce,hrnek->hrnck", attention, key_part, precision=highest
    )
    span_end = cumulative[..., -1:]
    scaled_keys = jnp.exp(span_end - cumulative)[..., None] * key_blocks
    transit = jnp.exp(span_end)[..., None] * jnp.eye(DK, dtype=jnp.float32) - jnp.einsum(
        "hrnck,hrnce->hrnke", scaled_keys, key_part, precision=highest
    )
    inject = jnp.einsum("hrnck,hrncv->hrnkv", scaled_keys, value_part, precision=highest)
    transit_seq = jnp.moveaxis(transit, 2, 0)
    inject_seq = jnp.moveaxis(inject, 2, 0)
    identity = jnp.broadcast_to(jnp.eye(DK, dtype=jnp.float32), (key_heads, ratio_heads, DK, DK))
    zero_state = jnp.zeros((key_heads, ratio_heads, DK, DV), jnp.float32)

    def sweep_spans(carried, span_in):
        prefix, state_now = carried
        transit_now, inject_now = span_in
        return (
            (apply_map(transit_now, prefix), apply_map(transit_now, state_now) + inject_now),
            None,
        )

    (total_map, local_end), ignored = lax.scan(
        sweep_spans, (identity, zero_state), (transit_seq, inject_seq)
    )

    seq_size = lax.axis_size("seq")
    seq_index = lax.axis_index("seq")
    prefix_map, prefix_end = total_map, local_end
    distance = 1
    while distance < seq_size:
        if 2 * distance < seq_size:
            earlier_map, earlier_end = shifted(
                jnp.stack([prefix_map, prefix_end]), "seq", distance
            )
            prefix_end = apply_map(prefix_map, earlier_end) + prefix_end
            prefix_map = jnp.where(
                seq_index >= distance, apply_map(prefix_map, earlier_map), prefix_map
            )
        else:
            earlier_end = shifted(prefix_end, "seq", distance)
            prefix_end = apply_map(prefix_map, earlier_end) + prefix_end
        distance *= 2
    incoming = shifted(prefix_end, "seq", 1)

    def replay(state_now, span_in):
        transit_now, inject_now, coupling_now, local_now = span_in
        span_out = (
            jnp.einsum("hrck,hrkv->hrcv", coupling_now, state_now, precision=highest) + local_now
        )
        return (apply_map(transit_now, state_now) + inject_now, span_out)

    ignored_state, outputs = lax.scan(
        replay,
        incoming,
        (transit_seq, inject_seq, jnp.moveaxis(coupling, 2, 0), jnp.moveaxis(local_out, 2, 0)),
    )
    return outputs


def shards(
    query_proj,
    key_proj,
    value_proj,
    gate_proj,
    strength,
    log_decay,
    conv_query,
    conv_key,
    conv_value,
    norm_gain,
    out_weight,
):
    local_rows = query_proj.shape[0]
    rim_width = conv_query.shape[0] - 1
    before_query, before_key, before_value = shifted(
        (
            query_proj[local_rows - rim_width :],
            key_proj[local_rows - rim_width :],
            value_proj[local_rows - rim_width :],
        ),
        "seq",
        1,
    )
    key_heads = key_proj.shape[1] // DK
    value_heads = value_proj.shape[1] // DV
    ratio_heads = value_heads // key_heads
    spans = local_rows // SPAN
    queries = conv_silu(query_proj, before_query, conv_query)
    key_rows = conv_silu(key_proj, before_key, conv_key).reshape(local_rows, key_heads, DK)
    key_rows = key_rows / jnp.sqrt(jnp.sum(key_rows * key_rows, axis=-1, keepdims=True) + epsilon)
    values = conv_silu(value_proj, before_value, conv_value)
    query_blocks = queries.reshape(spans, SPAN, key_heads, DK).transpose(2, 0, 1, 3)[:, None]
    key_blocks = key_rows.reshape(spans, SPAN, key_heads, DK).transpose(2, 0, 1, 3)[:, None]
    value_blocks = values.reshape(spans, SPAN, key_heads, ratio_heads, DV).transpose(2, 3, 0, 1, 4)
    strength_blocks = strength.reshape(key_heads, ratio_heads, spans, SPAN)
    decay_blocks = log_decay.reshape(key_heads, ratio_heads, spans, SPAN)
    parts = [
        recurrence(
            query_blocks[group : group + 1],
            key_blocks[group : group + 1],
            value_blocks[group : group + 1],
            strength_blocks[group : group + 1],
            decay_blocks[group : group + 1],
        )
        for group in range(key_heads)
    ]
    outputs = jnp.concatenate(parts, axis=1)
    core_out = jnp.moveaxis(outputs, 0, 2)
    core_out = core_out.transpose(2, 3, 0, 1, 4).reshape(local_rows, value_heads, DV)
    gate_values = gate_proj.astype(jnp.float32).reshape(local_rows, value_heads, DV)
    scale_rows = lax.rsqrt(jnp.mean(core_out * core_out, axis=-1, keepdims=True) + epsilon)
    normed = core_out * scale_rows * norm_gain.astype(jnp.float32) * jax.nn.silu(gate_values)
    hidden = normed.reshape(local_rows, value_heads * DV).astype(jnp.bfloat16)
    partial_sum = jnp.dot(hidden, out_weight, preferred_element_type=jnp.float32).astype(
        jnp.bfloat16
    )
    head_size = lax.axis_size("head")
    pieces = lax.all_to_all(
        partial_sum.reshape(head_size, local_rows // head_size, partial_sum.shape[1]),
        "head",
        0,
        0,
    )
    return jnp.sum(pieces.astype(jnp.float32), axis=0).astype(jnp.bfloat16)


def solution(mesh):
    placed = (
        P("seq", "head"),
        P("seq", "head"),
        P("seq", "head"),
        P("seq", "head"),
        P("head", "seq"),
        P("head", "seq"),
        P(None, "head"),
        P(None, "head"),
        P(None, "head"),
        P(),
        P("head", None),
    )
    return jax.shard_map(
        shards, mesh=mesh, in_specs=placed, out_specs=P(("seq", "head"), None), check_vma=False
    )
```

```python
import jax
import jax.numpy as jnp
from jax import lax
from jax.sharding import PartitionSpec as P

DK = 128
DV = 128
SPAN = 128


epsilon = 1e-06
highest = lax.Precision.HIGHEST


def shifted(array, axis, by):
    length = lax.axis_size(axis)
    pairs = [(i, i + by) for i in range(length) if 0 <= i + by < length]
    return lax.ppermute(array, axis, pairs)


def conv_silu(signal, before, weights):
    length = signal.shape[0]
    padded = jnp.concatenate([before, signal], axis=0).astype(jnp.float32)
    conv_taps = weights.astype(jnp.float32)
    summed = jnp.zeros(signal.shape, jnp.float32)
    for offset in range(conv_taps.shape[0]):
        summed = summed + conv_taps[offset] * padded[offset : offset + length]
    return jax.nn.silu(summed)


def unit_lower_inverse(system):
    size = system.shape[-1]
    rows = jnp.arange(size)[:, None]
    cols = jnp.arange(size)[None, :]
    inverse = jnp.broadcast_to(jnp.eye(size, dtype=system.dtype), system.shape)
    width = 1
    while width < size:
        same_block = (rows // (2 * width)) == (cols // (2 * width))
        lower_half = (rows // width) > (cols // width)
        coupling = jnp.where(same_block & lower_half, system, 0.0)
        correction = jnp.einsum(
            "...ij,...jk->...ik",
            jnp.einsum("...ij,...jk->...ik", inverse, coupling, precision=highest),
            inverse,
            precision=highest,
        )
        inverse = jnp.where(same_block & lower_half, -correction, inverse)
        width *= 2
    return inverse


def apply_map(matrix, state_now):
    return jnp.einsum("hrke,hrev->hrkv", matrix, state_now, precision=highest)


def recurrence(query_blocks, key_blocks, value_blocks, strength_blocks, decay_blocks):
    key_heads, ratio_heads = value_blocks.shape[:2]
    cumulative = jnp.cumsum(decay_blocks, axis=-1)
    positions = jnp.arange(SPAN)
    inclusive = positions[:, None] >= positions[None, :]
    strictly = positions[:, None] > positions[None, :]
    log_gaps = cumulative[..., :, None] - cumulative[..., None, :]
    decays = jnp.where(inclusive, jnp.exp(jnp.where(inclusive, log_gaps, 0.0)), 0.0)
    key_key = jnp.einsum("hxnck,hxnek->hxnce", key_blocks, key_blocks, precision=highest)
    query_key = jnp.einsum("hxnck,hxnek->hxnce", query_blocks, key_blocks, precision=highest)
    lower_part = jnp.where(strictly, strength_blocks[..., None] * decays * key_key, 0.0)
    system = lower_part + jnp.eye(SPAN, dtype=jnp.float32)
    right_side = jnp.concatenate(
        [
            strength_blocks[..., None] * value_blocks,
            (strength_blocks * jnp.exp(cumulative))[..., None] * key_blocks,
        ],
        axis=-1,
    )
    solved = jnp.einsum(
        "...ij,...jk->...ik", unit_lower_inverse(system), right_side, precision=highest
    )
    value_part = solved[..., :DV]
    key_part = solved[..., DV:]
    attention = decays * query_key
    local_out = jnp.einsum("hrnce,hrnev->hrncv", attention, value_part, precision=highest)
    coupling = jnp.exp(cumulative)[..., None] * query_blocks - jnp.einsum(
        "hrnce,hrnek->hrnck", attention, key_part, precision=highest
    )
    span_end = cumulative[..., -1:]
    scaled_keys = jnp.exp(span_end - cumulative)[..., None] * key_blocks
    transit = jnp.exp(span_end)[..., None] * jnp.eye(DK, dtype=jnp.float32) - jnp.einsum(
        "hrnck,hrnce->hrnke", scaled_keys, key_part, precision=highest
    )
    inject = jnp.einsum("hrnck,hrncv->hrnkv", scaled_keys, value_part, precision=highest)
    transit_seq = jnp.moveaxis(transit, 2, 0)
    inject_seq = jnp.moveaxis(inject, 2, 0)
    identity = jnp.broadcast_to(jnp.eye(DK, dtype=jnp.float32), (key_heads, ratio_heads, DK, DK))
    zero_state = jnp.zeros((key_heads, ratio_heads, DK, DV), jnp.float32)

    def sweep_spans(carried, span_in):
        prefix, state_now = carried
        transit_now, inject_now = span_in
        return (
            (apply_map(transit_now, prefix), apply_map(transit_now, state_now) + inject_now),
            None,
        )

    (total_map, local_end), ignored = lax.scan(
        sweep_spans, (identity, zero_state), (transit_seq, inject_seq)
    )

    seq_size = lax.axis_size("seq")
    seq_index = lax.axis_index("seq")
    prefix_map, prefix_end = total_map, local_end
    distance = 1
    while distance < seq_size:
        if 2 * distance < seq_size:
            earlier_map, earlier_end = shifted(
                jnp.stack([prefix_map, prefix_end]).astype(jnp.bfloat16), "seq", distance
            ).astype(jnp.float32)
            prefix_end = apply_map(prefix_map, earlier_end) + prefix_end
            prefix_map = jnp.where(
                seq_index >= distance, apply_map(prefix_map, earlier_map), prefix_map
            )
        else:
            earlier_end = shifted(prefix_end.astype(jnp.bfloat16), "seq", distance).astype(
                jnp.float32
            )
            prefix_end = apply_map(prefix_map, earlier_end) + prefix_end
        distance *= 2
    incoming = shifted(prefix_end.astype(jnp.bfloat16), "seq", 1).astype(jnp.float32)

    def replay(state_now, span_in):
        transit_now, inject_now, coupling_now, local_now = span_in
        span_out = (
            jnp.einsum("hrck,hrkv->hrcv", coupling_now, state_now, precision=highest) + local_now
        )
        return (apply_map(transit_now, state_now) + inject_now, span_out)

    ignored_state, outputs = lax.scan(
        replay,
        incoming,
        (transit_seq, inject_seq, jnp.moveaxis(coupling, 2, 0), jnp.moveaxis(local_out, 2, 0)),
    )
    return outputs


def shards(
    query_proj,
    key_proj,
    value_proj,
    gate_proj,
    strength,
    log_decay,
    conv_query,
    conv_key,
    conv_value,
    norm_gain,
    out_weight,
):
    local_rows = query_proj.shape[0]
    rim_width = conv_query.shape[0] - 1
    before_query, before_key, before_value = shifted(
        (
            query_proj[local_rows - rim_width :],
            key_proj[local_rows - rim_width :],
            value_proj[local_rows - rim_width :],
        ),
        "seq",
        1,
    )
    key_heads = key_proj.shape[1] // DK
    value_heads = value_proj.shape[1] // DV
    ratio_heads = value_heads // key_heads
    spans = local_rows // SPAN
    queries = conv_silu(query_proj, before_query, conv_query)
    key_rows = conv_silu(key_proj, before_key, conv_key).reshape(local_rows, key_heads, DK)
    key_rows = key_rows / jnp.sqrt(jnp.sum(key_rows * key_rows, axis=-1, keepdims=True) + epsilon)
    values = conv_silu(value_proj, before_value, conv_value)
    query_blocks = queries.reshape(spans, SPAN, key_heads, DK).transpose(2, 0, 1, 3)[:, None]
    key_blocks = key_rows.reshape(spans, SPAN, key_heads, DK).transpose(2, 0, 1, 3)[:, None]
    value_blocks = values.reshape(spans, SPAN, key_heads, ratio_heads, DV).transpose(2, 3, 0, 1, 4)
    strength_blocks = strength.reshape(key_heads, ratio_heads, spans, SPAN)
    decay_blocks = log_decay.reshape(key_heads, ratio_heads, spans, SPAN)
    parts = [
        recurrence(
            query_blocks[group : group + 1],
            key_blocks[group : group + 1],
            value_blocks[group : group + 1],
            strength_blocks[group : group + 1],
            decay_blocks[group : group + 1],
        )
        for group in range(key_heads)
    ]
    outputs = jnp.concatenate(parts, axis=1)
    core_out = jnp.moveaxis(outputs, 0, 2)
    core_out = core_out.transpose(2, 3, 0, 1, 4).reshape(local_rows, value_heads, DV)
    gate_values = gate_proj.astype(jnp.float32).reshape(local_rows, value_heads, DV)
    scale_rows = lax.rsqrt(jnp.mean(core_out * core_out, axis=-1, keepdims=True) + epsilon)
    normed = core_out * scale_rows * norm_gain.astype(jnp.float32) * jax.nn.silu(gate_values)
    hidden = normed.reshape(local_rows, value_heads * DV).astype(jnp.bfloat16)
    partial_sum = jnp.dot(hidden, out_weight, preferred_element_type=jnp.float32).astype(
        jnp.bfloat16
    )
    head_size = lax.axis_size("head")
    pieces = lax.all_to_all(
        partial_sum.reshape(head_size, local_rows // head_size, partial_sum.shape[1]),
        "head",
        0,
        0,
    )
    return jnp.sum(pieces.astype(jnp.float32), axis=0).astype(jnp.bfloat16)


def solution(mesh):
    placed = (
        P("seq", "head"),
        P("seq", "head"),
        P("seq", "head"),
        P("seq", "head"),
        P("head", "seq"),
        P("head", "seq"),
        P(None, "head"),
        P(None, "head"),
        P(None, "head"),
        P(),
        P("head", None),
    )
    return jax.shard_map(
        shards, mesh=mesh, in_specs=placed, out_specs=P(("seq", "head"), None), check_vma=False
    )
```

```python
import jax
import jax.numpy as jnp
from jax import lax
from jax.sharding import PartitionSpec as P

DK = 128
DV = 128
SPAN = 128


epsilon = 1e-06
highest = lax.Precision.HIGHEST


def shifted(array, axis, by):
    length = lax.axis_size(axis)
    pairs = [(i, i + by) for i in range(length) if 0 <= i + by < length]
    return lax.ppermute(array, axis, pairs)


def conv_silu(signal, before, weights):
    length = signal.shape[0]
    padded = jnp.concatenate([before, signal], axis=0).astype(jnp.float32)
    conv_taps = weights.astype(jnp.float32)
    summed = jnp.zeros(signal.shape, jnp.float32)
    for offset in range(conv_taps.shape[0]):
        summed = summed + conv_taps[offset] * padded[offset : offset + length]
    return jax.nn.silu(summed)


def unit_lower_inverse(system):
    size = system.shape[-1]
    rows = jnp.arange(size)[:, None]
    cols = jnp.arange(size)[None, :]
    inverse = jnp.broadcast_to(jnp.eye(size, dtype=system.dtype), system.shape)
    width = 1
    while width < size:
        same_block = (rows // (2 * width)) == (cols // (2 * width))
        lower_half = (rows // width) > (cols // width)
        coupling = jnp.where(same_block & lower_half, system, 0.0)
        correction = jnp.einsum(
            "...ij,...jk->...ik",
            jnp.einsum("...ij,...jk->...ik", inverse, coupling, precision=highest),
            inverse,
            precision=highest,
        )
        inverse = jnp.where(same_block & lower_half, -correction, inverse)
        width *= 2
    return inverse


def apply_map(matrix, state_now):
    return jnp.einsum("hrke,hrev->hrkv", matrix, state_now, precision=highest)


def chunk_maps(query_blocks, key_blocks, value_blocks, strength_blocks, decay_blocks):
    cumulative = jnp.cumsum(decay_blocks, axis=-1)
    positions = jnp.arange(SPAN)
    inclusive = positions[:, None] >= positions[None, :]
    strictly = positions[:, None] > positions[None, :]
    log_gaps = cumulative[..., :, None] - cumulative[..., None, :]
    decays = jnp.where(inclusive, jnp.exp(jnp.where(inclusive, log_gaps, 0.0)), 0.0)
    key_key = jnp.einsum("hxnck,hxnek->hxnce", key_blocks, key_blocks, precision=highest)
    query_key = jnp.einsum("hxnck,hxnek->hxnce", query_blocks, key_blocks, precision=highest)
    lower_part = jnp.where(strictly, strength_blocks[..., None] * decays * key_key, 0.0)
    system = lower_part + jnp.eye(SPAN, dtype=jnp.float32)
    right_side = jnp.concatenate(
        [
            strength_blocks[..., None] * value_blocks,
            (strength_blocks * jnp.exp(cumulative))[..., None] * key_blocks,
        ],
        axis=-1,
    )
    solved = jnp.einsum(
        "...ij,...jk->...ik", unit_lower_inverse(system), right_side, precision=highest
    )
    value_part = solved[..., :DV]
    key_part = solved[..., DV:]
    attention = decays * query_key
    local_out = jnp.einsum("hrnce,hrnev->hrncv", attention, value_part, precision=highest)
    coupling = jnp.exp(cumulative)[..., None] * query_blocks - jnp.einsum(
        "hrnce,hrnek->hrnck", attention, key_part, precision=highest
    )
    span_end = cumulative[..., -1:]
    scaled_keys = jnp.exp(span_end - cumulative)[..., None] * key_blocks
    transit = jnp.exp(span_end)[..., None] * jnp.eye(DK, dtype=jnp.float32) - jnp.einsum(
        "hrnck,hrnce->hrnke", scaled_keys, key_part, precision=highest
    )
    inject = jnp.einsum("hrnck,hrncv->hrnkv", scaled_keys, value_part, precision=highest)
    return transit, inject, coupling, local_out


def relay_group(transit, inject, coupling, local_out):
    key_heads, ratio_heads = transit.shape[:2]
    transit_seq = jnp.moveaxis(transit, 2, 0)
    inject_seq = jnp.moveaxis(inject, 2, 0)
    identity = jnp.broadcast_to(jnp.eye(DK, dtype=jnp.float32), (key_heads, ratio_heads, DK, DK))
    zero_state = jnp.zeros((key_heads, ratio_heads, DK, DV), jnp.float32)

    def sweep_spans(carried, span_in):
        prefix, state_now = carried
        transit_now, inject_now = span_in
        return (
            (apply_map(transit_now, prefix), apply_map(transit_now, state_now) + inject_now),
            None,
        )

    (total_map, local_end), ignored = lax.scan(
        sweep_spans, (identity, zero_state), (transit_seq, inject_seq)
    )

    seq_size = lax.axis_size("seq")
    seq_index = lax.axis_index("seq")
    prefix_map, prefix_end = total_map, local_end
    distance = 1
    while distance < seq_size:
        if 2 * distance < seq_size:
            earlier_map, earlier_end = shifted(
                jnp.stack([prefix_map, prefix_end]).astype(jnp.bfloat16), "seq", distance
            ).astype(jnp.float32)
            prefix_end = apply_map(prefix_map, earlier_end) + prefix_end
            prefix_map = jnp.where(
                seq_index >= distance, apply_map(prefix_map, earlier_map), prefix_map
            )
        else:
            earlier_end = shifted(prefix_end.astype(jnp.bfloat16), "seq", distance).astype(
                jnp.float32
            )
            prefix_end = apply_map(prefix_map, earlier_end) + prefix_end
        distance *= 2
    incoming = shifted(prefix_end.astype(jnp.bfloat16), "seq", 1).astype(jnp.float32)

    def replay(state_now, span_in):
        transit_now, inject_now, coupling_now, local_now = span_in
        span_out = (
            jnp.einsum("hrck,hrkv->hrcv", coupling_now, state_now, precision=highest) + local_now
        )
        return (apply_map(transit_now, state_now) + inject_now, span_out)

    ignored_state, outputs = lax.scan(
        replay,
        incoming,
        (transit_seq, inject_seq, jnp.moveaxis(coupling, 2, 0), jnp.moveaxis(local_out, 2, 0)),
    )
    return outputs


def shards(
    query_proj,
    key_proj,
    value_proj,
    gate_proj,
    strength,
    log_decay,
    conv_query,
    conv_key,
    conv_value,
    norm_gain,
    out_weight,
):
    local_rows = query_proj.shape[0]
    rim_width = conv_query.shape[0] - 1
    before_query, before_key, before_value = shifted(
        (
            query_proj[local_rows - rim_width :],
            key_proj[local_rows - rim_width :],
            value_proj[local_rows - rim_width :],
        ),
        "seq",
        1,
    )
    key_heads = key_proj.shape[1] // DK
    value_heads = value_proj.shape[1] // DV
    ratio_heads = value_heads // key_heads
    spans = local_rows // SPAN
    queries = conv_silu(query_proj, before_query, conv_query)
    key_rows = conv_silu(key_proj, before_key, conv_key).reshape(local_rows, key_heads, DK)
    key_rows = key_rows / jnp.sqrt(jnp.sum(key_rows * key_rows, axis=-1, keepdims=True) + epsilon)
    values = conv_silu(value_proj, before_value, conv_value)
    query_blocks = queries.reshape(spans, SPAN, key_heads, DK).transpose(2, 0, 1, 3)[:, None]
    key_blocks = key_rows.reshape(spans, SPAN, key_heads, DK).transpose(2, 0, 1, 3)[:, None]
    value_blocks = values.reshape(spans, SPAN, key_heads, ratio_heads, DV).transpose(2, 3, 0, 1, 4)
    strength_blocks = strength.reshape(key_heads, ratio_heads, spans, SPAN)
    decay_blocks = log_decay.reshape(key_heads, ratio_heads, spans, SPAN)
    maps = chunk_maps(query_blocks, key_blocks, value_blocks, strength_blocks, decay_blocks)
    parts = [
        relay_group(*[piece[group : group + 1] for piece in maps]) for group in range(key_heads)
    ]
    outputs = jnp.concatenate(parts, axis=1)
    core_out = jnp.moveaxis(outputs, 0, 2)
    core_out = core_out.transpose(2, 3, 0, 1, 4).reshape(local_rows, value_heads, DV)
    gate_values = gate_proj.astype(jnp.float32).reshape(local_rows, value_heads, DV)
    scale_rows = lax.rsqrt(jnp.mean(core_out * core_out, axis=-1, keepdims=True) + epsilon)
    normed = core_out * scale_rows * norm_gain.astype(jnp.float32) * jax.nn.silu(gate_values)
    hidden = normed.reshape(local_rows, value_heads * DV).astype(jnp.bfloat16)
    partial_sum = jnp.dot(hidden, out_weight, preferred_element_type=jnp.float32).astype(
        jnp.bfloat16
    )
    head_size = lax.axis_size("head")
    head_index = lax.axis_index("head")
    pieces = partial_sum.reshape(head_size, local_rows // head_size, partial_sum.shape[1])
    summed = pieces[head_index].astype(jnp.float32)
    for hop in range(1, head_size):
        outgoing = pieces[(head_index + hop) % head_size]
        pairs = [(i, (i + hop) % head_size) for i in range(head_size)]
        summed = summed + lax.ppermute(outgoing, "head", pairs).astype(jnp.float32)
    return summed.astype(jnp.bfloat16)


def solution(mesh):
    placed = (
        P("seq", "head"),
        P("seq", "head"),
        P("seq", "head"),
        P("seq", "head"),
        P("head", "seq"),
        P("head", "seq"),
        P(None, "head"),
        P(None, "head"),
        P(None, "head"),
        P(),
        P("head", None),
    )
    return jax.shard_map(
        shards, mesh=mesh, in_specs=placed, out_specs=P(("seq", "head"), None), check_vma=False
    )
```

```python
import jax
import jax.numpy as jnp
from jax import lax
from jax.sharding import PartitionSpec as P

DK = 128
DV = 128
SPAN = 128


epsilon = 1e-06
highest = lax.Precision.HIGHEST


def shifted(array, axis, by):
    length = lax.axis_size(axis)
    pairs = [(i, i + by) for i in range(length) if 0 <= i + by < length]
    return lax.ppermute(array, axis, pairs)


def conv_silu(signal, before, weights):
    length = signal.shape[0]
    padded = jnp.concatenate([before, signal], axis=0).astype(jnp.float32)
    conv_taps = weights.astype(jnp.float32)
    summed = jnp.zeros(signal.shape, jnp.float32)
    for offset in range(conv_taps.shape[0]):
        summed = summed + conv_taps[offset] * padded[offset : offset + length]
    return jax.nn.silu(summed)


def unit_lower_inverse(system):
    size = system.shape[-1]
    rows = jnp.arange(size)[:, None]
    cols = jnp.arange(size)[None, :]
    inverse = jnp.broadcast_to(jnp.eye(size, dtype=system.dtype), system.shape)
    width = 1
    while width < size:
        same_block = (rows // (2 * width)) == (cols // (2 * width))
        lower_half = (rows // width) > (cols // width)
        coupling = jnp.where(same_block & lower_half, system, 0.0)
        correction = jnp.einsum(
            "...ij,...jk->...ik",
            jnp.einsum("...ij,...jk->...ik", inverse, coupling, precision=highest),
            inverse,
            precision=highest,
        )
        inverse = jnp.where(same_block & lower_half, -correction, inverse)
        width *= 2
    return inverse


def apply_map(matrix, state_now):
    return jnp.einsum("hrke,hrev->hrkv", matrix, state_now, precision=highest)


def chunk_maps(query_blocks, key_blocks, value_blocks, strength_blocks, decay_blocks):
    cumulative = jnp.cumsum(decay_blocks, axis=-1)
    positions = jnp.arange(SPAN)
    inclusive = positions[:, None] >= positions[None, :]
    strictly = positions[:, None] > positions[None, :]
    log_gaps = cumulative[..., :, None] - cumulative[..., None, :]
    decays = jnp.where(inclusive, jnp.exp(jnp.where(inclusive, log_gaps, 0.0)), 0.0)
    key_key = jnp.einsum("hxnck,hxnek->hxnce", key_blocks, key_blocks, precision=highest)
    query_key = jnp.einsum("hxnck,hxnek->hxnce", query_blocks, key_blocks, precision=highest)
    lower_part = jnp.where(strictly, strength_blocks[..., None] * decays * key_key, 0.0)
    system = lower_part + jnp.eye(SPAN, dtype=jnp.float32)
    right_side = jnp.concatenate(
        [
            strength_blocks[..., None] * value_blocks,
            (strength_blocks * jnp.exp(cumulative))[..., None] * key_blocks,
        ],
        axis=-1,
    )
    solved = jnp.einsum(
        "...ij,...jk->...ik", unit_lower_inverse(system), right_side, precision=highest
    )
    value_part = solved[..., :DV]
    key_part = solved[..., DV:]
    attention = decays * query_key
    local_out = jnp.einsum("hrnce,hrnev->hrncv", attention, value_part, precision=highest)
    coupling = jnp.exp(cumulative)[..., None] * query_blocks - jnp.einsum(
        "hrnce,hrnek->hrnck", attention, key_part, precision=highest
    )
    span_end = cumulative[..., -1:]
    scaled_keys = jnp.exp(span_end - cumulative)[..., None] * key_blocks
    transit = jnp.exp(span_end)[..., None] * jnp.eye(DK, dtype=jnp.float32) - jnp.einsum(
        "hrnck,hrnce->hrnke", scaled_keys, key_part, precision=highest
    )
    inject = jnp.einsum("hrnck,hrncv->hrnkv", scaled_keys, value_part, precision=highest)
    return transit, inject, coupling, local_out


def relay_group(transit, inject, coupling, local_out):
    key_heads, ratio_heads = transit.shape[:2]
    transit_seq = jnp.moveaxis(transit, 2, 0)
    inject_seq = jnp.moveaxis(inject, 2, 0)
    identity = jnp.broadcast_to(jnp.eye(DK, dtype=jnp.float32), (key_heads, ratio_heads, DK, DK))
    zero_state = jnp.zeros((key_heads, ratio_heads, DK, DV), jnp.float32)

    def sweep_spans(carried, span_in):
        prefix, state_now = carried
        transit_now, inject_now = span_in
        return (
            (apply_map(transit_now, prefix), apply_map(transit_now, state_now) + inject_now),
            None,
        )

    (total_map, local_end), ignored = lax.scan(
        sweep_spans, (identity, zero_state), (transit_seq, inject_seq), unroll=True
    )

    seq_size = lax.axis_size("seq")
    seq_index = lax.axis_index("seq")
    prefix_map, prefix_end = total_map, local_end
    distance = 1
    while distance < seq_size:
        if 2 * distance < seq_size:
            earlier_map, earlier_end = shifted(
                jnp.stack([prefix_map, prefix_end]).astype(jnp.bfloat16), "seq", distance
            ).astype(jnp.float32)
            prefix_end = apply_map(prefix_map, earlier_end) + prefix_end
            prefix_map = jnp.where(
                seq_index >= distance, apply_map(prefix_map, earlier_map), prefix_map
            )
        else:
            earlier_end = shifted(prefix_end.astype(jnp.bfloat16), "seq", distance).astype(
                jnp.float32
            )
            prefix_end = apply_map(prefix_map, earlier_end) + prefix_end
        distance *= 2
    incoming = shifted(prefix_end.astype(jnp.bfloat16), "seq", 1).astype(jnp.float32)

    def replay(state_now, span_in):
        transit_now, inject_now, coupling_now, local_now = span_in
        span_out = (
            jnp.einsum("hrck,hrkv->hrcv", coupling_now, state_now, precision=highest) + local_now
        )
        return (apply_map(transit_now, state_now) + inject_now, span_out)

    ignored_state, outputs = lax.scan(
        replay,
        incoming,
        (transit_seq, inject_seq, jnp.moveaxis(coupling, 2, 0), jnp.moveaxis(local_out, 2, 0)),
        unroll=True,
    )
    return outputs


def shards(
    query_proj,
    key_proj,
    value_proj,
    gate_proj,
    strength,
    log_decay,
    conv_query,
    conv_key,
    conv_value,
    norm_gain,
    out_weight,
):
    local_rows = query_proj.shape[0]
    rim_width = conv_query.shape[0] - 1
    before_query, before_key, before_value = shifted(
        (
            query_proj[local_rows - rim_width :],
            key_proj[local_rows - rim_width :],
            value_proj[local_rows - rim_width :],
        ),
        "seq",
        1,
    )
    key_heads = key_proj.shape[1] // DK
    value_heads = value_proj.shape[1] // DV
    ratio_heads = value_heads // key_heads
    spans = local_rows // SPAN
    queries = conv_silu(query_proj, before_query, conv_query)
    key_rows = conv_silu(key_proj, before_key, conv_key).reshape(local_rows, key_heads, DK)
    key_rows = key_rows / jnp.sqrt(jnp.sum(key_rows * key_rows, axis=-1, keepdims=True) + epsilon)
    values = conv_silu(value_proj, before_value, conv_value)
    query_blocks = queries.reshape(spans, SPAN, key_heads, DK).transpose(2, 0, 1, 3)[:, None]
    key_blocks = key_rows.reshape(spans, SPAN, key_heads, DK).transpose(2, 0, 1, 3)[:, None]
    value_blocks = values.reshape(spans, SPAN, key_heads, ratio_heads, DV).transpose(2, 3, 0, 1, 4)
    strength_blocks = strength.reshape(key_heads, ratio_heads, spans, SPAN)
    decay_blocks = log_decay.reshape(key_heads, ratio_heads, spans, SPAN)
    maps = chunk_maps(query_blocks, key_blocks, value_blocks, strength_blocks, decay_blocks)
    parts = [
        relay_group(*[piece[group : group + 1] for piece in maps]) for group in range(key_heads)
    ]
    outputs = jnp.concatenate(parts, axis=1)
    core_out = jnp.moveaxis(outputs, 0, 2)
    core_out = core_out.transpose(2, 3, 0, 1, 4).reshape(local_rows, value_heads, DV)
    gate_values = gate_proj.astype(jnp.float32).reshape(local_rows, value_heads, DV)
    scale_rows = lax.rsqrt(jnp.mean(core_out * core_out, axis=-1, keepdims=True) + epsilon)
    normed = core_out * scale_rows * norm_gain.astype(jnp.float32) * jax.nn.silu(gate_values)
    hidden = normed.reshape(local_rows, value_heads * DV).astype(jnp.bfloat16)
    partial_sum = jnp.dot(hidden, out_weight, preferred_element_type=jnp.float32)
    head_size = lax.axis_size("head")
    head_index = lax.axis_index("head")
    chips = head_size // 2
    pieces = partial_sum.reshape(chips, 2, local_rows // head_size, partial_sum.shape[1])
    parity = head_index % 2
    chip = head_index // 2
    sibling_pairs = [(i, i ^ 1) for i in range(head_size)]
    from_sibling = lax.ppermute(pieces[:, 1 - parity].astype(jnp.bfloat16), "head", sibling_pairs)
    chip_sum = (pieces[:, parity] + from_sibling.astype(jnp.float32)).astype(jnp.bfloat16)
    summed = chip_sum[chip].astype(jnp.float32)
    for hop in range(1, chips):
        outgoing = chip_sum[(chip + hop) % chips]
        pairs = [(i, (i + 2 * hop) % head_size) for i in range(head_size)]
        summed = summed + lax.ppermute(outgoing, "head", pairs).astype(jnp.float32)
    return summed.astype(jnp.bfloat16)


def solution(mesh):
    placed = (
        P("seq", "head"),
        P("seq", "head"),
        P("seq", "head"),
        P("seq", "head"),
        P("head", "seq"),
        P("head", "seq"),
        P(None, "head"),
        P(None, "head"),
        P(None, "head"),
        P(),
        P("head", None),
    )
    return jax.shard_map(
        shards, mesh=mesh, in_specs=placed, out_specs=P(("seq", "head"), None), check_vma=False
    )
```

```python
import jax
import jax.numpy as jnp
from jax import lax
from jax.sharding import PartitionSpec as P

DK = 128
DV = 128
SPAN = 128


epsilon = 1e-06
highest = lax.Precision.HIGHEST


def shifted(array, axis, by):
    length = lax.axis_size(axis)
    pairs = [(i, i + by) for i in range(length) if 0 <= i + by < length]
    return lax.ppermute(array, axis, pairs)


def conv_silu(signal, before, weights):
    length = signal.shape[0]
    padded = jnp.concatenate([before, signal], axis=0).astype(jnp.float32)
    conv_taps = weights.astype(jnp.float32)
    summed = jnp.zeros(signal.shape, jnp.float32)
    for offset in range(conv_taps.shape[0]):
        summed = summed + conv_taps[offset] * padded[offset : offset + length]
    return jax.nn.silu(summed)


def unit_lower_inverse(system):
    size = system.shape[-1]
    rows = jnp.arange(size)[:, None]
    cols = jnp.arange(size)[None, :]
    inverse = jnp.broadcast_to(jnp.eye(size, dtype=system.dtype), system.shape)
    width = 1
    while width < size:
        same_block = (rows // (2 * width)) == (cols // (2 * width))
        lower_half = (rows // width) > (cols // width)
        coupling = jnp.where(same_block & lower_half, system, 0.0)
        correction = jnp.einsum(
            "...ij,...jk->...ik",
            jnp.einsum("...ij,...jk->...ik", inverse, coupling, precision=highest),
            inverse,
            precision=highest,
        )
        inverse = jnp.where(same_block & lower_half, -correction, inverse)
        width *= 2
    return inverse


def apply_map(matrix, state_now):
    return jnp.einsum("hrke,hrev->hrkv", matrix, state_now, precision=highest)


def chunk_maps(query_blocks, key_blocks, value_blocks, strength_blocks, decay_blocks):
    cumulative = jnp.cumsum(decay_blocks, axis=-1)
    positions = jnp.arange(SPAN)
    inclusive = positions[:, None] >= positions[None, :]
    strictly = positions[:, None] > positions[None, :]
    log_gaps = cumulative[..., :, None] - cumulative[..., None, :]
    decays = jnp.where(inclusive, jnp.exp(jnp.where(inclusive, log_gaps, 0.0)), 0.0)
    key_key = jnp.einsum("hxnck,hxnek->hxnce", key_blocks, key_blocks, precision=highest)
    query_key = jnp.einsum("hxnck,hxnek->hxnce", query_blocks, key_blocks, precision=highest)
    lower_part = jnp.where(strictly, strength_blocks[..., None] * decays * key_key, 0.0)
    system = lower_part + jnp.eye(SPAN, dtype=jnp.float32)
    right_side = jnp.concatenate(
        [
            strength_blocks[..., None] * value_blocks,
            (strength_blocks * jnp.exp(cumulative))[..., None] * key_blocks,
        ],
        axis=-1,
    )
    solved = jnp.einsum(
        "...ij,...jk->...ik", unit_lower_inverse(system), right_side, precision=highest
    )
    value_part = solved[..., :DV]
    key_part = solved[..., DV:]
    attention = decays * query_key
    local_out = jnp.einsum("hrnce,hrnev->hrncv", attention, value_part, precision=highest)
    coupling = jnp.exp(cumulative)[..., None] * query_blocks - jnp.einsum(
        "hrnce,hrnek->hrnck", attention, key_part, precision=highest
    )
    span_end = cumulative[..., -1:]
    scaled_keys = jnp.exp(span_end - cumulative)[..., None] * key_blocks
    transit = jnp.exp(span_end)[..., None] * jnp.eye(DK, dtype=jnp.float32) - jnp.einsum(
        "hrnck,hrnce->hrnke", scaled_keys, key_part, precision=highest
    )
    inject = jnp.einsum("hrnck,hrncv->hrnkv", scaled_keys, value_part, precision=highest)
    return transit, inject, coupling, local_out


def relay_group(transit, inject, coupling, local_out):
    key_heads, ratio_heads = transit.shape[:2]
    transit_seq = jnp.moveaxis(transit, 2, 0)
    inject_seq = jnp.moveaxis(inject, 2, 0)
    identity = jnp.broadcast_to(jnp.eye(DK, dtype=jnp.float32), (key_heads, ratio_heads, DK, DK))
    zero_state = jnp.zeros((key_heads, ratio_heads, DK, DV), jnp.float32)

    def sweep_spans(carried, span_in):
        prefix, state_now = carried
        transit_now, inject_now = span_in
        return (
            (apply_map(transit_now, prefix), apply_map(transit_now, state_now) + inject_now),
            None,
        )

    (total_map, local_end), ignored = lax.scan(
        sweep_spans, (identity, zero_state), (transit_seq, inject_seq), unroll=True
    )

    seq_size = lax.axis_size("seq")
    seq_index = lax.axis_index("seq")
    prefix_map, prefix_end = total_map, local_end
    distance = 1
    while distance < seq_size:
        if 2 * distance < seq_size:
            earlier_map, earlier_end = shifted(
                jnp.stack([prefix_map, prefix_end]).astype(jnp.bfloat16), "seq", distance
            ).astype(jnp.float32)
            prefix_end = apply_map(prefix_map, earlier_end) + prefix_end
            prefix_map = jnp.where(
                seq_index >= distance, apply_map(prefix_map, earlier_map), prefix_map
            )
        else:
            earlier_end = shifted(prefix_end.astype(jnp.bfloat16), "seq", distance).astype(
                jnp.float32
            )
            prefix_end = apply_map(prefix_map, earlier_end) + prefix_end
        distance *= 2
    incoming = shifted(prefix_end.astype(jnp.bfloat16), "seq", 1).astype(jnp.float32)

    def replay(state_now, span_in):
        transit_now, inject_now, coupling_now, local_now = span_in
        span_out = (
            jnp.einsum("hrck,hrkv->hrcv", coupling_now, state_now, precision=highest) + local_now
        )
        return (apply_map(transit_now, state_now) + inject_now, span_out)

    ignored_state, outputs = lax.scan(
        replay,
        incoming,
        (transit_seq, inject_seq, jnp.moveaxis(coupling, 2, 0), jnp.moveaxis(local_out, 2, 0)),
        unroll=True,
    )
    return outputs


def shards(
    query_proj,
    key_proj,
    value_proj,
    gate_proj,
    strength,
    log_decay,
    conv_query,
    conv_key,
    conv_value,
    norm_gain,
    out_weight,
):
    local_rows = query_proj.shape[0]
    rim_width = conv_query.shape[0] - 1
    query_width = query_proj.shape[1]
    key_width = key_proj.shape[1]
    before_all = shifted(
        jnp.concatenate(
            [
                query_proj[local_rows - rim_width :],
                key_proj[local_rows - rim_width :],
                value_proj[local_rows - rim_width :],
            ],
            axis=1,
        ),
        "seq",
        1,
    )
    before_query = before_all[:, :query_width]
    before_key = before_all[:, query_width : query_width + key_width]
    before_value = before_all[:, query_width + key_width :]
    key_heads = key_proj.shape[1] // DK
    value_heads = value_proj.shape[1] // DV
    ratio_heads = value_heads // key_heads
    spans = local_rows // SPAN
    queries = conv_silu(query_proj, before_query, conv_query)
    key_rows = conv_silu(key_proj, before_key, conv_key).reshape(local_rows, key_heads, DK)
    key_rows = key_rows / jnp.sqrt(jnp.sum(key_rows * key_rows, axis=-1, keepdims=True) + epsilon)
    values = conv_silu(value_proj, before_value, conv_value)
    query_blocks = queries.reshape(spans, SPAN, key_heads, DK).transpose(2, 0, 1, 3)[:, None]
    key_blocks = key_rows.reshape(spans, SPAN, key_heads, DK).transpose(2, 0, 1, 3)[:, None]
    value_blocks = values.reshape(spans, SPAN, key_heads, ratio_heads, DV).transpose(2, 3, 0, 1, 4)
    strength_blocks = strength.reshape(key_heads, ratio_heads, spans, SPAN)
    decay_blocks = log_decay.reshape(key_heads, ratio_heads, spans, SPAN)
    maps = chunk_maps(query_blocks, key_blocks, value_blocks, strength_blocks, decay_blocks)
    parts = [
        relay_group(*[piece[group : group + 1] for piece in maps]) for group in range(key_heads)
    ]
    outputs = jnp.concatenate(parts, axis=1)
    core_out = jnp.moveaxis(outputs, 0, 2)
    core_out = core_out.transpose(2, 3, 0, 1, 4).reshape(local_rows, value_heads, DV)
    gate_values = gate_proj.astype(jnp.float32).reshape(local_rows, value_heads, DV)
    scale_rows = lax.rsqrt(jnp.mean(core_out * core_out, axis=-1, keepdims=True) + epsilon)
    normed = core_out * scale_rows * norm_gain.astype(jnp.float32) * jax.nn.silu(gate_values)
    hidden = normed.reshape(local_rows, value_heads * DV).astype(jnp.bfloat16)
    partial_sum = jnp.dot(hidden, out_weight, preferred_element_type=jnp.float32)
    head_size = lax.axis_size("head")
    head_index = lax.axis_index("head")
    chips = head_size // 2
    pieces = partial_sum.reshape(chips, 2, local_rows // head_size, partial_sum.shape[1])
    parity = head_index % 2
    chip = head_index // 2
    sibling_pairs = [(i, i ^ 1) for i in range(head_size)]
    from_sibling = lax.ppermute(pieces[:, 1 - parity].astype(jnp.bfloat16), "head", sibling_pairs)
    chip_sum = (pieces[:, parity] + from_sibling.astype(jnp.float32)).astype(jnp.bfloat16)
    summed = chip_sum[chip].astype(jnp.float32)
    for hop in range(1, chips):
        outgoing = chip_sum[(chip + hop) % chips]
        pairs = [(i, (i + 2 * hop) % head_size) for i in range(head_size)]
        summed = summed + lax.ppermute(outgoing, "head", pairs).astype(jnp.float32)
    return summed.astype(jnp.bfloat16)


def solution(mesh):
    placed = (
        P("seq", "head"),
        P("seq", "head"),
        P("seq", "head"),
        P("seq", "head"),
        P("head", "seq"),
        P("head", "seq"),
        P(None, "head"),
        P(None, "head"),
        P(None, "head"),
        P(),
        P("head", None),
    )
    return jax.shard_map(
        shards, mesh=mesh, in_specs=placed, out_specs=P(("seq", "head"), None), check_vma=False
    )
```

```python
import jax
import jax.numpy as jnp
from jax import lax
from jax.sharding import PartitionSpec as P

DK = 128
DV = 128
SPAN = 128


epsilon = 1e-06
highest = lax.Precision.HIGHEST


def shifted(array, axis, by):
    length = lax.axis_size(axis)
    pairs = [(i, i + by) for i in range(length) if 0 <= i + by < length]
    return lax.ppermute(array, axis, pairs)


def conv_silu(signal, before, weights):
    length = signal.shape[0]
    padded = jnp.concatenate([before, signal], axis=0).astype(jnp.float32)
    conv_taps = weights.astype(jnp.float32)
    summed = jnp.zeros(signal.shape, jnp.float32)
    for offset in range(conv_taps.shape[0]):
        summed = summed + conv_taps[offset] * padded[offset : offset + length]
    return jax.nn.silu(summed)


def unit_lower_inverse(system):
    size = system.shape[-1]
    rows = jnp.arange(size)[:, None]
    cols = jnp.arange(size)[None, :]
    inverse = jnp.broadcast_to(jnp.eye(size, dtype=system.dtype), system.shape)
    width = 1
    while width < size:
        same_block = (rows // (2 * width)) == (cols // (2 * width))
        lower_half = (rows // width) > (cols // width)
        coupling = jnp.where(same_block & lower_half, system, 0.0)
        correction = jnp.einsum(
            "...ij,...jk->...ik",
            jnp.einsum("...ij,...jk->...ik", inverse, coupling, precision=highest),
            inverse,
            precision=highest,
        )
        inverse = jnp.where(same_block & lower_half, -correction, inverse)
        width *= 2
    return inverse


def apply_map(matrix, state_now):
    return jnp.einsum("hrke,hrev->hrkv", matrix, state_now, precision=highest)


def chunk_maps(query_blocks, key_blocks, value_blocks, strength_blocks, decay_blocks):
    cumulative = jnp.cumsum(decay_blocks, axis=-1)
    positions = jnp.arange(SPAN)
    inclusive = positions[:, None] >= positions[None, :]
    strictly = positions[:, None] > positions[None, :]
    log_gaps = cumulative[..., :, None] - cumulative[..., None, :]
    decays = jnp.where(inclusive, jnp.exp(jnp.where(inclusive, log_gaps, 0.0)), 0.0)
    key_key = jnp.einsum("hxnck,hxnek->hxnce", key_blocks, key_blocks, precision=highest)
    query_key = jnp.einsum("hxnck,hxnek->hxnce", query_blocks, key_blocks, precision=highest)
    lower_part = jnp.where(strictly, strength_blocks[..., None] * decays * key_key, 0.0)
    system = lower_part + jnp.eye(SPAN, dtype=jnp.float32)
    right_side = jnp.concatenate(
        [
            strength_blocks[..., None] * value_blocks,
            (strength_blocks * jnp.exp(cumulative))[..., None] * key_blocks,
        ],
        axis=-1,
    )
    solved = jnp.einsum(
        "...ij,...jk->...ik", unit_lower_inverse(system), right_side, precision=highest
    )
    value_part = solved[..., :DV]
    key_part = solved[..., DV:]
    attention = decays * query_key
    local_out = jnp.einsum("hrnce,hrnev->hrncv", attention, value_part, precision=highest)
    coupling = jnp.exp(cumulative)[..., None] * query_blocks - jnp.einsum(
        "hrnce,hrnek->hrnck", attention, key_part, precision=highest
    )
    span_end = cumulative[..., -1:]
    scaled_keys = jnp.exp(span_end - cumulative)[..., None] * key_blocks
    transit = jnp.exp(span_end)[..., None] * jnp.eye(DK, dtype=jnp.float32) - jnp.einsum(
        "hrnck,hrnce->hrnke", scaled_keys, key_part, precision=highest
    )
    inject = jnp.einsum("hrnck,hrncv->hrnkv", scaled_keys, value_part, precision=highest)
    return transit, inject, coupling, local_out


def relay_group(transit, inject, coupling, local_out):
    key_heads, ratio_heads = transit.shape[:2]
    transit_seq = jnp.moveaxis(transit, 2, 0)
    inject_seq = jnp.moveaxis(inject, 2, 0)
    identity = jnp.broadcast_to(jnp.eye(DK, dtype=jnp.float32), (key_heads, ratio_heads, DK, DK))
    zero_state = jnp.zeros((key_heads, ratio_heads, DK, DV), jnp.float32)

    def sweep_spans(carried, span_in):
        prefix, state_now = carried
        transit_now, inject_now = span_in
        return (
            (apply_map(transit_now, prefix), apply_map(transit_now, state_now) + inject_now),
            None,
        )

    (total_map, local_end), ignored = lax.scan(
        sweep_spans, (identity, zero_state), (transit_seq, inject_seq), unroll=True
    )

    seq_size = lax.axis_size("seq")
    seq_index = lax.axis_index("seq")
    prefix_map, prefix_end = total_map, local_end
    distance = 1
    while distance < seq_size:
        if 2 * distance < seq_size:
            earlier_map, earlier_end = shifted(
                jnp.stack([prefix_map, prefix_end]).astype(jnp.bfloat16), "seq", distance
            ).astype(jnp.float32)
            prefix_end = apply_map(prefix_map, earlier_end) + prefix_end
            prefix_map = jnp.where(
                seq_index >= distance, apply_map(prefix_map, earlier_map), prefix_map
            )
        else:
            earlier_end = shifted(prefix_end.astype(jnp.bfloat16), "seq", distance).astype(
                jnp.float32
            )
            prefix_end = apply_map(prefix_map, earlier_end) + prefix_end
        distance *= 2
    incoming = shifted(prefix_end.astype(jnp.bfloat16), "seq", 1).astype(jnp.float32)

    def replay(state_now, span_in):
        transit_now, inject_now, coupling_now, local_now = span_in
        span_out = (
            jnp.einsum("hrck,hrkv->hrcv", coupling_now, state_now, precision=highest) + local_now
        )
        return (apply_map(transit_now, state_now) + inject_now, span_out)

    ignored_state, outputs = lax.scan(
        replay,
        incoming,
        (transit_seq, inject_seq, jnp.moveaxis(coupling, 2, 0), jnp.moveaxis(local_out, 2, 0)),
        unroll=True,
    )
    return outputs


def shards(
    query_proj,
    key_proj,
    value_proj,
    gate_proj,
    strength,
    log_decay,
    conv_query,
    conv_key,
    conv_value,
    norm_gain,
    out_weight,
):
    local_rows = query_proj.shape[0]
    rim_width = conv_query.shape[0] - 1
    query_width = query_proj.shape[1]
    key_width = key_proj.shape[1]
    before_all = shifted(
        jnp.concatenate(
            [
                query_proj[local_rows - rim_width :],
                key_proj[local_rows - rim_width :],
                value_proj[local_rows - rim_width :],
            ],
            axis=1,
        ),
        "seq",
        1,
    )
    before_query = before_all[:, :query_width]
    before_key = before_all[:, query_width : query_width + key_width]
    before_value = before_all[:, query_width + key_width :]
    key_heads = key_proj.shape[1] // DK
    value_heads = value_proj.shape[1] // DV
    ratio_heads = value_heads // key_heads
    spans = local_rows // SPAN
    queries = conv_silu(query_proj, before_query, conv_query)
    key_rows = conv_silu(key_proj, before_key, conv_key).reshape(local_rows, key_heads, DK)
    key_rows = key_rows / jnp.sqrt(jnp.sum(key_rows * key_rows, axis=-1, keepdims=True) + epsilon)
    values = conv_silu(value_proj, before_value, conv_value)
    query_blocks = queries.reshape(spans, SPAN, key_heads, DK).transpose(2, 0, 1, 3)[:, None]
    key_blocks = key_rows.reshape(spans, SPAN, key_heads, DK).transpose(2, 0, 1, 3)[:, None]
    value_blocks = values.reshape(spans, SPAN, key_heads, ratio_heads, DV).transpose(2, 3, 0, 1, 4)
    strength_blocks = strength.reshape(key_heads, ratio_heads, spans, SPAN)
    decay_blocks = log_decay.reshape(key_heads, ratio_heads, spans, SPAN)
    maps = chunk_maps(query_blocks, key_blocks, value_blocks, strength_blocks, decay_blocks)
    outputs = relay_group(*maps)
    core_out = jnp.moveaxis(outputs, 0, 2)
    core_out = core_out.transpose(2, 3, 0, 1, 4).reshape(local_rows, value_heads, DV)
    gate_values = gate_proj.astype(jnp.float32).reshape(local_rows, value_heads, DV)
    scale_rows = lax.rsqrt(jnp.mean(core_out * core_out, axis=-1, keepdims=True) + epsilon)
    normed = core_out * scale_rows * norm_gain.astype(jnp.float32) * jax.nn.silu(gate_values)
    hidden = normed.reshape(local_rows, value_heads * DV).astype(jnp.bfloat16)
    partial_sum = jnp.dot(hidden, out_weight, preferred_element_type=jnp.float32)
    head_size = lax.axis_size("head")
    head_index = lax.axis_index("head")
    chips = head_size // 2
    pieces = partial_sum.reshape(chips, 2, local_rows // head_size, partial_sum.shape[1])
    parity = head_index % 2
    chip = head_index // 2
    sibling_pairs = [(i, i ^ 1) for i in range(head_size)]
    from_sibling = lax.ppermute(pieces[:, 1 - parity].astype(jnp.bfloat16), "head", sibling_pairs)
    chip_sum = (pieces[:, parity] + from_sibling.astype(jnp.float32)).astype(jnp.bfloat16)
    summed = chip_sum[chip].astype(jnp.float32)
    for hop in range(1, chips):
        outgoing = chip_sum[(chip + hop) % chips]
        pairs = [(i, (i + 2 * hop) % head_size) for i in range(head_size)]
        summed = summed + lax.ppermute(outgoing, "head", pairs).astype(jnp.float32)
    return summed.astype(jnp.bfloat16)


def solution(mesh):
    placed = (
        P("seq", "head"),
        P("seq", "head"),
        P("seq", "head"),
        P("seq", "head"),
        P("head", "seq"),
        P("head", "seq"),
        P(None, "head"),
        P(None, "head"),
        P(None, "head"),
        P(),
        P("head", None),
    )
    return jax.shard_map(
        shards, mesh=mesh, in_specs=placed, out_specs=P(("seq", "head"), None), check_vma=False
    )
```

```python
import jax
import jax.numpy as jnp
from jax import lax
from jax.sharding import PartitionSpec as P

DK = 128
DV = 128
SPAN = 128


epsilon = 1e-06
highest = lax.Precision.HIGHEST


def shifted(array, axis, by):
    length = lax.axis_size(axis)
    pairs = [(i, i + by) for i in range(length) if 0 <= i + by < length]
    return lax.ppermute(array, axis, pairs)


def conv_silu(signal, before, weights):
    length = signal.shape[0]
    padded = jnp.concatenate([before, signal], axis=0).astype(jnp.float32)
    conv_taps = weights.astype(jnp.float32)
    summed = jnp.zeros(signal.shape, jnp.float32)
    for offset in range(conv_taps.shape[0]):
        summed = summed + conv_taps[offset] * padded[offset : offset + length]
    return jax.nn.silu(summed)


def unit_lower_inverse(system):
    size = system.shape[-1]
    rows = jnp.arange(size)[:, None]
    cols = jnp.arange(size)[None, :]
    inverse = jnp.broadcast_to(jnp.eye(size, dtype=system.dtype), system.shape)
    width = 1
    while width < size:
        same_block = (rows // (2 * width)) == (cols // (2 * width))
        lower_half = (rows // width) > (cols // width)
        coupling = jnp.where(same_block & lower_half, system, 0.0)
        correction = jnp.einsum(
            "...ij,...jk->...ik",
            jnp.einsum("...ij,...jk->...ik", inverse, coupling, precision=highest),
            inverse,
            precision=highest,
        )
        inverse = jnp.where(same_block & lower_half, -correction, inverse)
        width *= 2
    return inverse


def apply_map(matrix, state_now):
    return jnp.einsum("hrke,hrev->hrkv", matrix, state_now, precision=highest)


def chunk_maps(query_blocks, key_blocks, value_blocks, strength_blocks, decay_blocks):
    cumulative = jnp.cumsum(decay_blocks, axis=-1)
    positions = jnp.arange(SPAN)
    inclusive = positions[:, None] >= positions[None, :]
    strictly = positions[:, None] > positions[None, :]
    log_gaps = cumulative[..., :, None] - cumulative[..., None, :]
    decays = jnp.where(inclusive, jnp.exp(jnp.where(inclusive, log_gaps, 0.0)), 0.0)
    key_key = jnp.einsum("hxnck,hxnek->hxnce", key_blocks, key_blocks, precision=highest)
    query_key = jnp.einsum("hxnck,hxnek->hxnce", query_blocks, key_blocks, precision=highest)
    lower_part = jnp.where(strictly, strength_blocks[..., None] * decays * key_key, 0.0)
    system = lower_part + jnp.eye(SPAN, dtype=jnp.float32)
    right_side = jnp.concatenate(
        [
            strength_blocks[..., None] * value_blocks,
            (strength_blocks * jnp.exp(cumulative))[..., None] * key_blocks,
        ],
        axis=-1,
    )
    solved = jnp.einsum(
        "...ij,...jk->...ik", unit_lower_inverse(system), right_side, precision=highest
    )
    value_part = solved[..., :DV]
    key_part = solved[..., DV:]
    attention = decays * query_key
    local_out = jnp.einsum("hrnce,hrnev->hrncv", attention, value_part, precision=highest)
    coupling = jnp.exp(cumulative)[..., None] * query_blocks - jnp.einsum(
        "hrnce,hrnek->hrnck", attention, key_part, precision=highest
    )
    span_end = cumulative[..., -1:]
    scaled_keys = jnp.exp(span_end - cumulative)[..., None] * key_blocks
    transit = jnp.exp(span_end)[..., None] * jnp.eye(DK, dtype=jnp.float32) - jnp.einsum(
        "hrnck,hrnce->hrnke", scaled_keys, key_part, precision=highest
    )
    inject = jnp.einsum("hrnck,hrncv->hrnkv", scaled_keys, value_part, precision=highest)
    return transit, inject, coupling, local_out


def relay_group(transit, inject, coupling, local_out):
    key_heads, ratio_heads = transit.shape[:2]
    transit_seq = jnp.moveaxis(transit, 2, 0)
    inject_seq = jnp.moveaxis(inject, 2, 0)
    identity = jnp.broadcast_to(jnp.eye(DK, dtype=jnp.float32), (key_heads, ratio_heads, DK, DK))
    zero_state = jnp.zeros((key_heads, ratio_heads, DK, DV), jnp.float32)

    def sweep_spans(carried, span_in):
        prefix, state_now = carried
        transit_now, inject_now = span_in
        return (
            (apply_map(transit_now, prefix), apply_map(transit_now, state_now) + inject_now),
            None,
        )

    (total_map, local_end), ignored = lax.scan(
        sweep_spans, (identity, zero_state), (transit_seq, inject_seq), unroll=True
    )

    seq_size = lax.axis_size("seq")
    seq_index = lax.axis_index("seq")
    prefix_map, prefix_end = total_map, local_end
    distance = 1
    while 2 * distance < seq_size:
        earlier_map, earlier_end = shifted(
            jnp.stack([prefix_map, prefix_end]).astype(jnp.bfloat16), "seq", distance
        ).astype(jnp.float32)
        prefix_end = apply_map(prefix_map, earlier_end) + prefix_end
        prefix_map = jnp.where(
            seq_index >= distance, apply_map(prefix_map, earlier_map), prefix_map
        )
        distance *= 2
    last_map, last_end = shifted(
        jnp.stack([prefix_map, prefix_end]).astype(jnp.bfloat16), "seq", 1
    ).astype(jnp.float32)
    far_end = shifted(prefix_end.astype(jnp.bfloat16), "seq", distance + 1).astype(jnp.float32)
    incoming = apply_map(last_map, far_end) + last_end

    def replay(state_now, span_in):
        transit_now, inject_now, coupling_now, local_now = span_in
        span_out = (
            jnp.einsum("hrck,hrkv->hrcv", coupling_now, state_now, precision=highest) + local_now
        )
        return (apply_map(transit_now, state_now) + inject_now, span_out)

    ignored_state, outputs = lax.scan(
        replay,
        incoming,
        (transit_seq, inject_seq, jnp.moveaxis(coupling, 2, 0), jnp.moveaxis(local_out, 2, 0)),
        unroll=True,
    )
    return outputs


def shards(
    query_proj,
    key_proj,
    value_proj,
    gate_proj,
    strength,
    log_decay,
    conv_query,
    conv_key,
    conv_value,
    norm_gain,
    out_weight,
):
    local_rows = query_proj.shape[0]
    rim_width = conv_query.shape[0] - 1
    query_width = query_proj.shape[1]
    key_width = key_proj.shape[1]
    before_all = shifted(
        jnp.concatenate(
            [
                query_proj[local_rows - rim_width :],
                key_proj[local_rows - rim_width :],
                value_proj[local_rows - rim_width :],
            ],
            axis=1,
        ),
        "seq",
        1,
    )
    before_query = before_all[:, :query_width]
    before_key = before_all[:, query_width : query_width + key_width]
    before_value = before_all[:, query_width + key_width :]
    key_heads = key_proj.shape[1] // DK
    value_heads = value_proj.shape[1] // DV
    ratio_heads = value_heads // key_heads
    spans = local_rows // SPAN
    queries = conv_silu(query_proj, before_query, conv_query)
    key_rows = conv_silu(key_proj, before_key, conv_key).reshape(local_rows, key_heads, DK)
    key_rows = key_rows / jnp.sqrt(jnp.sum(key_rows * key_rows, axis=-1, keepdims=True) + epsilon)
    values = conv_silu(value_proj, before_value, conv_value)
    query_blocks = queries.reshape(spans, SPAN, key_heads, DK).transpose(2, 0, 1, 3)[:, None]
    key_blocks = key_rows.reshape(spans, SPAN, key_heads, DK).transpose(2, 0, 1, 3)[:, None]
    value_blocks = values.reshape(spans, SPAN, key_heads, ratio_heads, DV).transpose(2, 3, 0, 1, 4)
    strength_blocks = strength.reshape(key_heads, ratio_heads, spans, SPAN)
    decay_blocks = log_decay.reshape(key_heads, ratio_heads, spans, SPAN)
    maps = chunk_maps(query_blocks, key_blocks, value_blocks, strength_blocks, decay_blocks)
    parts = [
        relay_group(*[piece[group : group + 1] for piece in maps]) for group in range(key_heads)
    ]
    outputs = jnp.concatenate(parts, axis=1)
    core_out = jnp.moveaxis(outputs, 0, 2)
    core_out = core_out.transpose(2, 3, 0, 1, 4).reshape(local_rows, value_heads, DV)
    gate_values = gate_proj.astype(jnp.float32).reshape(local_rows, value_heads, DV)
    scale_rows = lax.rsqrt(jnp.mean(core_out * core_out, axis=-1, keepdims=True) + epsilon)
    normed = core_out * scale_rows * norm_gain.astype(jnp.float32) * jax.nn.silu(gate_values)
    hidden = normed.reshape(local_rows, value_heads * DV).astype(jnp.bfloat16)
    partial_sum = jnp.dot(hidden, out_weight, preferred_element_type=jnp.float32)
    head_size = lax.axis_size("head")
    head_index = lax.axis_index("head")
    chips = head_size // 2
    pieces = partial_sum.reshape(chips, 2, local_rows // head_size, partial_sum.shape[1])
    parity = head_index % 2
    chip = head_index // 2
    sibling_pairs = [(i, i ^ 1) for i in range(head_size)]
    from_sibling = lax.ppermute(pieces[:, 1 - parity].astype(jnp.bfloat16), "head", sibling_pairs)
    chip_sum = (pieces[:, parity] + from_sibling.astype(jnp.float32)).astype(jnp.bfloat16)
    summed = chip_sum[chip].astype(jnp.float32)
    for hop in range(1, chips):
        outgoing = chip_sum[(chip + hop) % chips]
        pairs = [(i, (i + 2 * hop) % head_size) for i in range(head_size)]
        summed = summed + lax.ppermute(outgoing, "head", pairs).astype(jnp.float32)
    return summed.astype(jnp.bfloat16)


def solution(mesh):
    placed = (
        P("seq", "head"),
        P("seq", "head"),
        P("seq", "head"),
        P("seq", "head"),
        P("head", "seq"),
        P("head", "seq"),
        P(None, "head"),
        P(None, "head"),
        P(None, "head"),
        P(),
        P("head", None),
    )
    return jax.shard_map(
        shards, mesh=mesh, in_specs=placed, out_specs=P(("seq", "head"), None), check_vma=False
    )
```

```python
import jax
import jax.numpy as jnp
from jax import lax
from jax.sharding import PartitionSpec as P

DK = 128
DV = 128
SPAN = 128


epsilon = 1e-06
highest = lax.Precision.HIGHEST


def shifted(array, axis, by):
    length = lax.axis_size(axis)
    pairs = [(i, i + by) for i in range(length) if 0 <= i + by < length]
    return lax.ppermute(array, axis, pairs)


def conv_silu(signal, before, weights):
    length = signal.shape[0]
    padded = jnp.concatenate([before, signal], axis=0).astype(jnp.float32)
    conv_taps = weights.astype(jnp.float32)
    summed = jnp.zeros(signal.shape, jnp.float32)
    for offset in range(conv_taps.shape[0]):
        summed = summed + conv_taps[offset] * padded[offset : offset + length]
    return jax.nn.silu(summed)


def unit_lower_inverse(system):
    size = system.shape[-1]
    rows = jnp.arange(size)[:, None]
    cols = jnp.arange(size)[None, :]
    inverse = jnp.broadcast_to(jnp.eye(size, dtype=system.dtype), system.shape)
    width = 1
    while width < size:
        same_block = (rows // (2 * width)) == (cols // (2 * width))
        lower_half = (rows // width) > (cols // width)
        coupling = jnp.where(same_block & lower_half, system, 0.0)
        correction = jnp.einsum(
            "...ij,...jk->...ik",
            jnp.einsum("...ij,...jk->...ik", inverse, coupling, precision=highest),
            inverse,
            precision=highest,
        )
        inverse = jnp.where(same_block & lower_half, -correction, inverse)
        width *= 2
    return inverse


def apply_map(matrix, state_now):
    return jnp.einsum("hrke,hrev->hrkv", matrix, state_now, precision=highest)


def chunk_maps(query_blocks, key_blocks, value_blocks, strength_blocks, decay_blocks):
    cumulative = jnp.cumsum(decay_blocks, axis=-1)
    positions = jnp.arange(SPAN)
    inclusive = positions[:, None] >= positions[None, :]
    strictly = positions[:, None] > positions[None, :]
    log_gaps = cumulative[..., :, None] - cumulative[..., None, :]
    decays = jnp.where(inclusive, jnp.exp(jnp.where(inclusive, log_gaps, 0.0)), 0.0)
    key_key = jnp.einsum("hxnck,hxnek->hxnce", key_blocks, key_blocks, precision=highest)
    query_key = jnp.einsum("hxnck,hxnek->hxnce", query_blocks, key_blocks, precision=highest)
    lower_part = jnp.where(strictly, strength_blocks[..., None] * decays * key_key, 0.0)
    system = lower_part + jnp.eye(SPAN, dtype=jnp.float32)
    right_side = jnp.concatenate(
        [
            strength_blocks[..., None] * value_blocks,
            (strength_blocks * jnp.exp(cumulative))[..., None] * key_blocks,
        ],
        axis=-1,
    )
    solved = jnp.einsum(
        "...ij,...jk->...ik", unit_lower_inverse(system), right_side, precision=highest
    )
    value_part = solved[..., :DV]
    key_part = solved[..., DV:]
    attention = decays * query_key
    local_out = jnp.einsum("hrnce,hrnev->hrncv", attention, value_part, precision=highest)
    coupling = jnp.exp(cumulative)[..., None] * query_blocks - jnp.einsum(
        "hrnce,hrnek->hrnck", attention, key_part, precision=highest
    )
    span_end = cumulative[..., -1:]
    scaled_keys = jnp.exp(span_end - cumulative)[..., None] * key_blocks
    transit = jnp.exp(span_end)[..., None] * jnp.eye(DK, dtype=jnp.float32) - jnp.einsum(
        "hrnck,hrnce->hrnke", scaled_keys, key_part, precision=highest
    )
    inject = jnp.einsum("hrnck,hrncv->hrnkv", scaled_keys, value_part, precision=highest)
    return transit, inject, coupling, local_out


def relay_group(transit, inject, coupling, local_out):
    key_heads, ratio_heads = transit.shape[:2]
    transit_seq = jnp.moveaxis(transit, 2, 0)
    inject_seq = jnp.moveaxis(inject, 2, 0)
    identity = jnp.broadcast_to(jnp.eye(DK, dtype=jnp.float32), (key_heads, ratio_heads, DK, DK))
    zero_state = jnp.zeros((key_heads, ratio_heads, DK, DV), jnp.float32)

    def sweep_spans(carried, span_in):
        prefix, state_now = carried
        transit_now, inject_now = span_in
        return (
            (apply_map(transit_now, prefix), apply_map(transit_now, state_now) + inject_now),
            None,
        )

    (total_map, local_end), ignored = lax.scan(
        sweep_spans, (identity, zero_state), (transit_seq, inject_seq), unroll=True
    )

    seq_size = lax.axis_size("seq")
    seq_index = lax.axis_index("seq")
    prefix_map, prefix_end = total_map, local_end
    distance = 1
    while 4 * distance < seq_size:
        earlier_map, earlier_end = shifted(
            jnp.stack([prefix_map, prefix_end]).astype(jnp.bfloat16), "seq", distance
        ).astype(jnp.float32)
        prefix_end = apply_map(prefix_map, earlier_end) + prefix_end
        prefix_map = jnp.where(
            seq_index >= distance, apply_map(prefix_map, earlier_map), prefix_map
        )
        distance *= 2
    windows = -(-seq_size // distance)
    incoming = shifted(
        prefix_end.astype(jnp.bfloat16), "seq", 1 + (windows - 1) * distance
    ).astype(jnp.float32)
    for window in range(windows - 2, -1, -1):
        window_map, window_end = shifted(
            jnp.stack([prefix_map, prefix_end]).astype(jnp.bfloat16), "seq", 1 + window * distance
        ).astype(jnp.float32)
        incoming = apply_map(window_map, incoming) + window_end

    def replay(state_now, span_in):
        transit_now, inject_now, coupling_now, local_now = span_in
        span_out = (
            jnp.einsum("hrck,hrkv->hrcv", coupling_now, state_now, precision=highest) + local_now
        )
        return (apply_map(transit_now, state_now) + inject_now, span_out)

    ignored_state, outputs = lax.scan(
        replay,
        incoming,
        (transit_seq, inject_seq, jnp.moveaxis(coupling, 2, 0), jnp.moveaxis(local_out, 2, 0)),
        unroll=True,
    )
    return outputs


def shards(
    query_proj,
    key_proj,
    value_proj,
    gate_proj,
    strength,
    log_decay,
    conv_query,
    conv_key,
    conv_value,
    norm_gain,
    out_weight,
):
    local_rows = query_proj.shape[0]
    rim_width = conv_query.shape[0] - 1
    query_width = query_proj.shape[1]
    key_width = key_proj.shape[1]
    before_all = shifted(
        jnp.concatenate(
            [
                query_proj[local_rows - rim_width :],
                key_proj[local_rows - rim_width :],
                value_proj[local_rows - rim_width :],
            ],
            axis=1,
        ),
        "seq",
        1,
    )
    before_query = before_all[:, :query_width]
    before_key = before_all[:, query_width : query_width + key_width]
    before_value = before_all[:, query_width + key_width :]
    key_heads = key_proj.shape[1] // DK
    value_heads = value_proj.shape[1] // DV
    ratio_heads = value_heads // key_heads
    spans = local_rows // SPAN
    queries = conv_silu(query_proj, before_query, conv_query)
    key_rows = conv_silu(key_proj, before_key, conv_key).reshape(local_rows, key_heads, DK)
    key_rows = key_rows / jnp.sqrt(jnp.sum(key_rows * key_rows, axis=-1, keepdims=True) + epsilon)
    values = conv_silu(value_proj, before_value, conv_value)
    query_blocks = queries.reshape(spans, SPAN, key_heads, DK).transpose(2, 0, 1, 3)[:, None]
    key_blocks = key_rows.reshape(spans, SPAN, key_heads, DK).transpose(2, 0, 1, 3)[:, None]
    value_blocks = values.reshape(spans, SPAN, key_heads, ratio_heads, DV).transpose(2, 3, 0, 1, 4)
    strength_blocks = strength.reshape(key_heads, ratio_heads, spans, SPAN)
    decay_blocks = log_decay.reshape(key_heads, ratio_heads, spans, SPAN)
    maps = chunk_maps(query_blocks, key_blocks, value_blocks, strength_blocks, decay_blocks)
    parts = [
        relay_group(*[piece[group : group + 1] for piece in maps]) for group in range(key_heads)
    ]
    outputs = jnp.concatenate(parts, axis=1)
    core_out = jnp.moveaxis(outputs, 0, 2)
    core_out = core_out.transpose(2, 3, 0, 1, 4).reshape(local_rows, value_heads, DV)
    gate_values = gate_proj.astype(jnp.float32).reshape(local_rows, value_heads, DV)
    scale_rows = lax.rsqrt(jnp.mean(core_out * core_out, axis=-1, keepdims=True) + epsilon)
    normed = core_out * scale_rows * norm_gain.astype(jnp.float32) * jax.nn.silu(gate_values)
    hidden = normed.reshape(local_rows, value_heads * DV).astype(jnp.bfloat16)
    partial_sum = jnp.dot(hidden, out_weight, preferred_element_type=jnp.float32)
    head_size = lax.axis_size("head")
    head_index = lax.axis_index("head")
    chips = head_size // 2
    pieces = partial_sum.reshape(chips, 2, local_rows // head_size, partial_sum.shape[1])
    parity = head_index % 2
    chip = head_index // 2
    sibling_pairs = [(i, i ^ 1) for i in range(head_size)]
    from_sibling = lax.ppermute(pieces[:, 1 - parity].astype(jnp.bfloat16), "head", sibling_pairs)
    chip_sum = (pieces[:, parity] + from_sibling.astype(jnp.float32)).astype(jnp.bfloat16)
    summed = chip_sum[chip].astype(jnp.float32)
    for hop in range(1, chips):
        outgoing = chip_sum[(chip + hop) % chips]
        pairs = [(i, (i + 2 * hop) % head_size) for i in range(head_size)]
        summed = summed + lax.ppermute(outgoing, "head", pairs).astype(jnp.float32)
    return summed.astype(jnp.bfloat16)


def solution(mesh):
    placed = (
        P("seq", "head"),
        P("seq", "head"),
        P("seq", "head"),
        P("seq", "head"),
        P("head", "seq"),
        P("head", "seq"),
        P(None, "head"),
        P(None, "head"),
        P(None, "head"),
        P(),
        P("head", None),
    )
    return jax.shard_map(
        shards, mesh=mesh, in_specs=placed, out_specs=P(("seq", "head"), None), check_vma=False
    )
```
